32 devices in a mesh: gx: 8 (over y, x, core), gy: 4 (over z).
Axes of the slice: x: 2, y: 2, z: 4, core: 2. Of those that a mesh axis runs over, the one named last changes fastest.
Arguments:
- bases: bfloat16 [3, 256, 128, 128], P(None, 'gx', 'gy'), may hold values from -6 to 6
- gains: bfloat16 [3, 256, 128, 128], P(None, 'gx', 'gy'), may hold values from -6 to 6
- scales: float32 [3, 256], replicated, may hold values from 0.3 to 3
Outputs:
- new_bases: bfloat16 [3, 256, 128, 128], P(None, 'gx', 'gy')
- new_cores: float32 [3, 8, 4, 128, 128], P(None, 'gx', 'gy')
The draws below stay inside these ranges and needn't reach their ends.
All inputs are finite; a program needn't handle non-finite values.
Results may differ from the reference program's by a relative error of at most 0.0012.
Values sent between devices are 32-bit elements; how exact they have to be, the bound alone decides.
No kernel may reach another device: no remote copies, remote signals or barrier semaphores. Data moves between devices by JAX's collectives and lax.ppermute only.
A program may use at most 64 MiB of HBM per device.

```python
import math
import jax
import jax.numpy as jnp
from jax import lax

R = 128
LEVELS = 3
NX = 256
NY = 128
N_GX = 8
N_GY = 4


def block_scale(key, shape, cuts, smallest, top_value):
    def one(dim, shards_of):
        heights = jax.random.uniform(jax.random.fold_in(jax.random.fold_in(key, 6), dim), (shards_of,), jnp.float32, smallest / len(cuts), top_value / len(cuts))
        return jnp.repeat(jnp.exp(heights), shape[dim] // shards_of).reshape((-1,) + (1,) * (len(shape) - dim - 1))

    factor_of = one(*cuts[0])
    for cut in cuts[1:]:
        factor_of = factor_of * one(*cut)
    return factor_of


def normal_values(own_key, dims, width, bound, split=(), kind=jnp.bfloat16):
    gain = block_scale(own_key, dims, split, -0.22, 0.18) if split else 1.0
    result = jax.random.normal(own_key, dims, jnp.float32) * width * gain
    return jnp.minimum(jnp.maximum(result, -bound), bound).astype(kind)


def setup_inputs(seed: int = 0) -> dict:
    seeds = jax.random.split(jax.random.key(seed), 4)
    bases = normal_values(seeds[0], (LEVELS, NX, NY, R), 1.0, 6.0, ((1, 8), (2, 4)))
    gains = normal_values(seeds[1], (LEVELS, NX, NY, R), 1.0, 6.0, ((1, 8), (2, 4)))
    scales = jnp.clip(jnp.exp(jax.random.uniform(seeds[2], (LEVELS, 2 * R), jnp.float32, math.log(0.3), math.log(3.0))), 0.3, 3.0)
    return dict(bases=bases, gains=gains, scales=scales)


def matmul(left, right):
    return jnp.dot(left, right, precision=lax.Precision.HIGHEST)

def inverse_lower(lower_factor):
    identity = jnp.eye(lower_factor.shape[0], dtype=lower_factor.dtype)
    return lax.linalg.triangular_solve(lower_factor, identity, left_side=True, lower=True)

def orthonormal(block):
    lower_factor = jnp.linalg.cholesky(matmul(block.T, block))
    return matmul(block, inverse_lower(lower_factor).T)

def first_factor(gram0, weights, n_rows):
    gram1 = weights[:, None] * gram0 * weights[None, :] / n_rows
    low1 = jnp.linalg.cholesky(gram1)
    t1 = weights[:, None] * inverse_lower(low1).T / math.sqrt(n_rows)
    return (low1, t1)

def truncate(low1, rank):
    upper = low1.T
    kernel = matmul(upper, upper.T)
    first_w = orthonormal(kernel[:, :rank])
    second_w = orthonormal(matmul(kernel, first_w))
    core = matmul(matmul(second_w.T, kernel), second_w)
    return (core, second_w)

def reference(bases, gains, scales):
    rank = bases.shape[-1]
    size_x = bases.shape[1]
    size_y = bases.shape[2]
    basis_list = []
    core_list = []
    for k in range(LEVELS):
        level = k
        parts_x = 2 ** ((level + 1) // 2)
        parts_y = 2 ** (level // 2)
        rows_x = size_x // parts_x
        rows_y = size_y // parts_y
        n_rows = rows_x * rows_y
        panel = jnp.concatenate([bases[k], gains[k]], axis=-1)
        panel = panel.reshape(parts_x, rows_x, parts_y, rows_y, 2 * rank)
        panel = panel.transpose(0, 2, 1, 3, 4).reshape(parts_x * parts_y, n_rows, 2 * rank)
        weights = scales[k]

        def node_update(block):
            gram0 = jnp.dot(block.T.astype(jnp.float32), block.astype(jnp.float32), preferred_element_type=jnp.float32)
            low1, t1 = first_factor(gram0, weights, n_rows)
            q1 = matmul(block.astype(jnp.float32), t1)
            core, second_w = truncate(low1, rank)
            basis = (matmul(q1, second_w) * math.sqrt(n_rows)).astype(jnp.bfloat16)
            return (basis, core)
        node_bases, node_cores = lax.map(node_update, panel)
        node_bases = node_bases.reshape(parts_x, parts_y, rows_x, rows_y, rank)
        basis_list.append(node_bases.transpose(0, 2, 1, 3, 4).reshape(size_x, size_y, rank))
        node_cores = node_cores.reshape(parts_x, parts_y, rank, rank)
        node_cores = jnp.repeat(node_cores, N_GX // parts_x, axis=0)
        core_list.append(jnp.repeat(node_cores, N_GY // parts_y, axis=1))
    return (jnp.stack(basis_list), jnp.stack(core_list))
```

```python
import math

import jax
import jax.numpy as jnp
from jax import lax
from jax.sharding import PartitionSpec as P

LEVELS = 3


def swapped(block, axis, apart):
    count = lax.axis_size(axis)
    route = []
    for low in range(count):
        high = low | 1 << apart
        if high != low and high < count:
            route += [(low, high), (high, low)]
    return lax.ppermute(block, axis, route)


def bmm(left, right):
    return jnp.einsum("bij,bjk->bik", left, right, precision=lax.Precision.HIGHEST)


def tr(block):
    return jnp.swapaxes(block, -1, -2)


def inverse_lower(lower_factor):
    identity = jnp.broadcast_to(jnp.eye(lower_factor.shape[-1], dtype=lower_factor.dtype), lower_factor.shape)
    return lax.linalg.triangular_solve(lower_factor, identity, left_side=True, lower=True)


def orthonormal(block):
    lower_factor = jnp.linalg.cholesky(bmm(tr(block), block))
    return bmm(block, tr(inverse_lower(lower_factor)))


def node_sum(total, groups):
    for bit in range(groups[0]):
        total = total + swapped(total, "gx", bit)
    for bit in range(groups[1]):
        total = total + swapped(total, "gy", bit)
    return total


def body(bases, gains, scales):
    rank = bases.shape[-1]
    local_rows = bases.shape[1] * bases.shape[2]
    bits_x = lax.axis_size("gx").bit_length() - 1
    bits_y = lax.axis_size("gy").bit_length() - 1
    panels = jnp.concatenate([bases, gains], axis=-1).reshape(LEVELS, local_rows, 2 * rank)
    grams = []
    sizes = []
    for k in range(LEVELS):
        groups = (bits_x - (k + 1) // 2, bits_y - k // 2)
        gram = jnp.dot(panels[k].T, panels[k], preferred_element_type=jnp.float32)
        grams.append(node_sum(gram, groups))
        sizes.append(local_rows * 2 ** (groups[0] + groups[1]))
    gram0 = jnp.stack(grams)
    n_rows = jnp.array(sizes, jnp.float32)[:, None, None]
    root_n = jnp.array([math.sqrt(n) for n in sizes], jnp.float32)[:, None, None]
    weights = scales[:, :, None]
    gram1 = weights * gram0 * tr(weights) / n_rows
    low1 = jnp.linalg.cholesky(gram1)
    t1 = weights * tr(inverse_lower(low1)) / root_n
    q1 = bmm(panels.astype(jnp.float32), t1)
    kernel = bmm(tr(low1), low1)
    first_w = orthonormal(kernel[:, :, :rank])
    second_w = orthonormal(bmm(kernel, first_w))
    core = bmm(bmm(tr(second_w), kernel), second_w)
    basis = (bmm(q1, second_w) * root_n).astype(jnp.bfloat16)
    return (basis.reshape(bases.shape), core.reshape(LEVELS, 1, 1, rank, rank))


def solution(mesh):
    in_specs = (P(None, "gx", "gy", None), P(None, "gx", "gy", None), P())
    out_specs = (P(None, "gx", "gy", None), P(None, "gx", "gy", None, None))
    return jax.shard_map(body, mesh=mesh, in_specs=in_specs, out_specs=out_specs, check_vma=False)
```

```python
import math

import jax
import jax.numpy as jnp
from jax import lax
from jax.experimental import pallas as pl
from jax.sharding import PartitionSpec as P

LEVELS = 3


def swapped(block, axis, apart):
    count = lax.axis_size(axis)
    route = []
    for low in range(count):
        high = low | 1 << apart
        if high != low and high < count:
            route += [(low, high), (high, low)]
    return lax.ppermute(block, axis, route)


def bmm(left, right):
    return jnp.einsum("bij,bjk->bik", left, right, precision=lax.Precision.HIGHEST)


def tr(block):
    return jnp.swapaxes(block, -1, -2)


def chol_inv_kernel(a_ref, lt_ref, w_ref):
    nb, n, _ = a_ref.shape
    nt = n // 8
    lane = lax.broadcasted_iota(jnp.int32, (1, n), 1)
    sub8 = lax.broadcasted_iota(jnp.int32, (8, 1), 0)
    rows8 = lax.broadcasted_iota(jnp.int32, (8, n), 0)
    cols8 = lax.broadcasted_iota(jnp.int32, (8, n), 1)
    a = [[a_ref[b, 8 * u:8 * u + 8, :] for u in range(nt)] for b in range(nb)]
    w = [[jnp.where(cols8 == rows8 + 8 * u, 1.0, 0.0).astype(jnp.float32) for u in range(nt)] for b in range(nb)]
    lt = [[None] * nt for b in range(nb)]
    for j in range(n):
        u0, s = divmod(j, 8)
        for b in range(nb):
            rowj = a[b][u0][s:s + 1, :]
            r = lax.rsqrt(rowj[:, j:j + 1])
            lrow = jnp.where(lane >= j, rowj * r, 0.0)
            if s == 0:
                lt[b][u0] = jnp.broadcast_to(lrow, (8, n))
            else:
                lt[b][u0] = jnp.where(sub8 == s, lrow, lt[b][u0])
            xrow = w[b][u0][s:s + 1, :] * r
            for u in range(u0, nt):
                col = a[b][u][:, j:j + 1] * r
                if u == u0:
                    col = jnp.where(sub8 >= s, col, 0.0)
                    wcol = col - jnp.where(sub8 == s, 1.0, 0.0)
                else:
                    wcol = col
                a[b][u] = a[b][u] - col * lrow
                w[b][u] = w[b][u] - wcol * xrow
    for b in range(nb):
        for u in range(nt):
            lt_ref[b, 8 * u:8 * u + 8, :] = lt[b][u]
            w_ref[b, 8 * u:8 * u + 8, :] = w[b][u]


def chol_inv(block):
    block = (block + tr(block)) / 2
    shape = jax.ShapeDtypeStruct(block.shape, jnp.float32)
    upper, inverse = pl.pallas_call(chol_inv_kernel, out_shape=(shape, shape))(block)
    return tr(upper), inverse


def chol_inv_blocked(block, half):
    block = (block + tr(block)) / 2
    low11, inv11 = chol_inv(block[:, :half, :half])
    low21 = bmm(block[:, half:, :half], tr(inv11))
    low22, inv22 = chol_inv(block[:, half:, half:] - bmm(low21, tr(low21)))
    inv21 = -bmm(inv22, bmm(low21, inv11))
    zero = jnp.zeros_like(low11)
    low = jnp.concatenate([jnp.concatenate([low11, zero], 2), jnp.concatenate([low21, low22], 2)], 1)
    inverse = jnp.concatenate([jnp.concatenate([inv11, zero], 2), jnp.concatenate([inv21, inv22], 2)], 1)
    return low, inverse


def orthonormal(block):
    _, inverse = chol_inv(bmm(tr(block), block))
    return bmm(block, tr(inverse))


def node_sum(total, groups):
    for bit in range(groups[0]):
        total = total + swapped(total, "gx", bit)
    for bit in range(groups[1]):
        total = total + swapped(total, "gy", bit)
    return total


def body(bases, gains, scales):
    rank = bases.shape[-1]
    local_rows = bases.shape[1] * bases.shape[2]
    bits_x = lax.axis_size("gx").bit_length() - 1
    bits_y = lax.axis_size("gy").bit_length() - 1
    panels = jnp.concatenate([bases, gains], axis=-1).reshape(LEVELS, local_rows, 2 * rank)
    grams = []
    sizes = []
    for k in range(LEVELS):
        groups = (bits_x - (k + 1) // 2, bits_y - k // 2)
        gram = jnp.dot(panels[k].T, panels[k], preferred_element_type=jnp.float32)
        grams.append(node_sum(gram, groups))
        sizes.append(local_rows * 2 ** (groups[0] + groups[1]))
    gram0 = jnp.stack(grams)
    n_rows = jnp.array(sizes, jnp.float32)[:, None, None]
    root_n = jnp.array([math.sqrt(n) for n in sizes], jnp.float32)[:, None, None]
    weights = scales[:, :, None]
    gram1 = weights * gram0 * tr(weights) / n_rows
    low1, inv1 = chol_inv_blocked(gram1, rank)
    t1 = weights * tr(inv1) / root_n
    q1 = bmm(panels.astype(jnp.float32), t1)
    kernel = bmm(tr(low1), low1)
    first_w = orthonormal(kernel[:, :, :rank])
    second_w = orthonormal(bmm(kernel, first_w))
    core = bmm(bmm(tr(second_w), kernel), second_w)
    basis = (bmm(q1, second_w) * root_n).astype(jnp.bfloat16)
    return (basis.reshape(bases.shape), core.reshape(LEVELS, 1, 1, rank, rank))


def solution(mesh):
    in_specs = (P(None, "gx", "gy", None), P(None, "gx", "gy", None), P())
    out_specs = (P(None, "gx", "gy", None), P(None, "gx", "gy", None, None))
    return jax.shard_map(body, mesh=mesh, in_specs=in_specs, out_specs=out_specs, check_vma=False)
```

```python
import math

import jax
import jax.numpy as jnp
from jax import lax
from jax.experimental import pallas as pl
from jax.sharding import Mesh, PartitionSpec as P

LEVELS = 3


def bmm(left, right):
    return jnp.einsum("bij,bjk->bik", left, right, precision=lax.Precision.HIGHEST)


def tr(block):
    return jnp.swapaxes(block, -1, -2)


def chol_inv_kernel(a_ref, lt_ref, w_ref):
    nb, n, _ = a_ref.shape
    nt = n // 8
    lane = lax.broadcasted_iota(jnp.int32, (1, n), 1)
    sub8 = lax.broadcasted_iota(jnp.int32, (8, 1), 0)
    rows8 = lax.broadcasted_iota(jnp.int32, (8, n), 0)
    cols8 = lax.broadcasted_iota(jnp.int32, (8, n), 1)
    a = [[a_ref[b, 8 * u:8 * u + 8, :] for u in range(nt)] for b in range(nb)]
    w = [[jnp.where(cols8 == rows8 + 8 * u, 1.0, 0.0).astype(jnp.float32) for u in range(nt)] for b in range(nb)]
    lt = [[None] * nt for b in range(nb)]
    for j in range(n):
        u0, s = divmod(j, 8)
        for b in range(nb):
            rowj = a[b][u0][s:s + 1, :]
            r = lax.rsqrt(rowj[:, j:j + 1])
            lrow = jnp.where(lane >= j, rowj * r, 0.0)
            if s == 0:
                lt[b][u0] = jnp.broadcast_to(lrow, (8, n))
            else:
                lt[b][u0] = jnp.where(sub8 == s, lrow, lt[b][u0])
            xrow = w[b][u0][s:s + 1, :] * r
            for u in range(u0, nt):
                col = a[b][u][:, j:j + 1] * r
                if u == u0:
                    col = jnp.where(sub8 >= s, col, 0.0)
                    wcol = col - jnp.where(sub8 == s, 1.0, 0.0)
                else:
                    wcol = col
                a[b][u] = a[b][u] - col * lrow
                w[b][u] = w[b][u] - wcol * xrow
    for b in range(nb):
        for u in range(nt):
            lt_ref[b, 8 * u:8 * u + 8, :] = lt[b][u]
            w_ref[b, 8 * u:8 * u + 8, :] = w[b][u]


def chol_inv(block):
    block = (block + tr(block)) / 2
    shape = jax.ShapeDtypeStruct(block.shape, jnp.float32)
    upper, inverse = pl.pallas_call(chol_inv_kernel, out_shape=(shape, shape))(block)
    return tr(upper), inverse


def chol_inv_blocked(block, half):
    block = (block + tr(block)) / 2
    low11, inv11 = chol_inv(block[:, :half, :half])
    low21 = bmm(block[:, half:, :half], tr(inv11))
    low22, inv22 = chol_inv(block[:, half:, half:] - bmm(low21, tr(low21)))
    inv21 = -bmm(inv22, bmm(low21, inv11))
    zero = jnp.zeros_like(low11)
    low = jnp.concatenate([jnp.concatenate([low11, zero], 2), jnp.concatenate([low21, low22], 2)], 1)
    inverse = jnp.concatenate([jnp.concatenate([inv11, zero], 2), jnp.concatenate([inv21, inv22], 2)], 1)
    return low, inverse


def orthonormal(block):
    _, inverse = chol_inv(bmm(tr(block), block))
    return bmm(block, tr(inverse))


def body(bases, gains, scales):
    rank = bases.shape[-1]
    local_rows = bases.shape[1] * bases.shape[2]
    panels = jnp.concatenate([bases, gains], axis=-1).reshape(LEVELS, local_rows, 2 * rank)
    grams = []
    sizes = []
    count = lax.axis_size(("xh", "xl", "yh", "yl"))
    for k in range(LEVELS):
        axes = ("xl",) if (k + 1) // 2 else ("xh", "xl")
        axes += ("yl",) if k // 2 else ("yh", "yl")
        gram = jnp.dot(panels[k].T, panels[k], preferred_element_type=jnp.float32)
        grams.append(lax.psum(gram, axes))
        sizes.append(local_rows * count // 2 ** ((k + 1) // 2 + k // 2))
    gram0 = jnp.stack(grams)
    n_rows = jnp.array(sizes, jnp.float32)[:, None, None]
    root_n = jnp.array([math.sqrt(n) for n in sizes], jnp.float32)[:, None, None]
    weights = scales[:, :, None]
    gram1 = weights * gram0 * tr(weights) / n_rows
    low1, inv1 = chol_inv_blocked(gram1, rank)
    t1 = weights * tr(inv1) / root_n
    q1 = bmm(panels.astype(jnp.float32), t1)
    kernel = bmm(tr(low1), low1)
    first_w = orthonormal(kernel[:, :, :rank])
    second_w = orthonormal(bmm(kernel, first_w))
    core = bmm(bmm(tr(second_w), kernel), second_w)
    basis = (bmm(q1, second_w) * root_n).astype(jnp.bfloat16)
    return (basis.reshape(bases.shape), core.reshape(LEVELS, 1, 1, rank, rank))


def solution(mesh):
    size_x, size_y = mesh.devices.shape
    split = Mesh(mesh.devices.reshape(2, size_x // 2, 2, size_y // 2), ("xh", "xl", "yh", "yl"))
    rows = P(None, ("xh", "xl"), ("yh", "yl"), None)
    in_specs = (rows, rows, P())
    out_specs = (rows, P(None, ("xh", "xl"), ("yh", "yl"), None, None))
    return jax.shard_map(body, mesh=split, in_specs=in_specs, out_specs=out_specs, check_vma=False)
```

```python
import math

import jax
import jax.numpy as jnp
from jax import lax
from jax.experimental import pallas as pl
from jax.sharding import PartitionSpec as P

LEVELS = 3


def swapped(block, axis, apart):
    count = lax.axis_size(axis)
    route = []
    for low in range(count):
        high = low | 1 << apart
        if high != low and high < count:
            route += [(low, high), (high, low)]
    return lax.ppermute(block, axis, route)


def bmm(left, right):
    return jnp.einsum("bij,bjk->bik", left, right, precision=lax.Precision.HIGHEST)


def tr(block):
    return jnp.swapaxes(block, -1, -2)


def chol_inv_kernel(a_ref, lt_ref, w_ref):
    nb, n, _ = a_ref.shape
    nt = n // 8
    lane = lax.broadcasted_iota(jnp.int32, (1, n), 1)
    sub8 = lax.broadcasted_iota(jnp.int32, (8, 1), 0)
    rows8 = lax.broadcasted_iota(jnp.int32, (8, n), 0)
    cols8 = lax.broadcasted_iota(jnp.int32, (8, n), 1)
    a = [[a_ref[b, 8 * u:8 * u + 8, :] for u in range(nt)] for b in range(nb)]
    w = [[jnp.where(cols8 == rows8 + 8 * u, 1.0, 0.0).astype(jnp.float32) for u in range(nt)] for b in range(nb)]
    lt = [[None] * nt for b in range(nb)]
    for j in range(n):
        u0, s = divmod(j, 8)
        for b in range(nb):
            rowj = a[b][u0][s:s + 1, :]
            r = lax.rsqrt(rowj[:, j:j + 1])
            lrow = jnp.where(lane >= j, rowj * r, 0.0)
            if s == 0:
                lt[b][u0] = jnp.broadcast_to(lrow, (8, n))
            else:
                lt[b][u0] = jnp.where(sub8 == s, lrow, lt[b][u0])
            xrow = w[b][u0][s:s + 1, :] * r
            for u in range(u0, nt):
                col = a[b][u][:, j:j + 1] * r
                if u == u0:
                    col = jnp.where(sub8 >= s, col, 0.0)
                    wcol = col - jnp.where(sub8 == s, 1.0, 0.0)
                else:
                    wcol = col
                a[b][u] = a[b][u] - col * lrow
                w[b][u] = w[b][u] - wcol * xrow
    for b in range(nb):
        for u in range(nt):
            lt_ref[b, 8 * u:8 * u + 8, :] = lt[b][u]
            w_ref[b, 8 * u:8 * u + 8, :] = w[b][u]


def chol_inv(block):
    block = (block + tr(block)) / 2
    shape = jax.ShapeDtypeStruct(block.shape, jnp.float32)
    upper, inverse = pl.pallas_call(chol_inv_kernel, out_shape=(shape, shape))(block)
    return tr(upper), inverse


def chol_inv_blocked(block, half):
    block = (block + tr(block)) / 2
    low11, inv11 = chol_inv(block[:, :half, :half])
    low21 = bmm(block[:, half:, :half], tr(inv11))
    low22, inv22 = chol_inv(block[:, half:, half:] - bmm(low21, tr(low21)))
    inv21 = -bmm(inv22, bmm(low21, inv11))
    zero = jnp.zeros_like(low11)
    low = jnp.concatenate([jnp.concatenate([low11, zero], 2), jnp.concatenate([low21, low22], 2)], 1)
    inverse = jnp.concatenate([jnp.concatenate([inv11, zero], 2), jnp.concatenate([inv21, inv22], 2)], 1)
    return low, inverse


def orthonormal(block):
    _, inverse = chol_inv(bmm(tr(block), block))
    return bmm(block, tr(inverse))


def round_orders(needs):
    best = [list(bits) for bits in needs]

    def search(left, round_no, orders, budget):
        if all(not bits for bits in left):
            return orders
        if budget[0] <= 0:
            return None
        budget[0] -= 1
        active = sorted((i for i in range(len(left)) if left[i]), key=lambda i: -len(left[i]))

        def place(pos, used, picks):
            if pos == len(active):
                new_left = [list(bits) for bits in left]
                new_orders = [list(order) for order in orders]
                for i, bit in picks:
                    new_left[i].remove(bit)
                    new_orders[i].append(bit)
                return search(new_left, round_no + 1, new_orders, budget)
            i = active[pos]
            for bit in left[i]:
                link = bit if bit[0] == "gx" else ("gy",)
                if link not in used:
                    found = place(pos + 1, used | {link}, picks + [(i, bit)])
                    if found:
                        return found
            return None

        return place(0, frozenset(), [])

    found = search([list(bits) for bits in needs], 0, [[] for _ in needs], [2000])
    return found if found else best


def node_sums(items, needs):
    orders = round_orders(needs)
    out = []
    for item, order in zip(items, orders):
        for axis, bit in order:
            item = item + swapped(item, axis, bit)
        out.append(item)
    return out


def pack(gram, rank):
    rows = lax.broadcasted_iota(jnp.int32, (rank, rank), 0)
    cols = lax.broadcasted_iota(jnp.int32, (rank, rank), 1)
    both = jnp.where(rows <= cols, gram[:rank, :rank], gram[rank:, rank:].T)
    diag = jnp.diagonal(gram[rank:, rank:])[None, :]
    pad = jnp.zeros((7, rank), gram.dtype)
    return jnp.concatenate([both, gram[:rank, rank:], diag, pad], axis=0)


def unpack(packed, rank):
    rows = lax.broadcasted_iota(jnp.int32, (rank, rank), 0)
    cols = lax.broadcasted_iota(jnp.int32, (rank, rank), 1)
    both = packed[:rank]
    cross = packed[rank:2 * rank]
    diag = packed[2 * rank]
    first = jnp.where(rows <= cols, both, both.T)
    second = jnp.where(rows > cols, both, jnp.where(rows == cols, diag[None, :], both.T))
    return jnp.concatenate([jnp.concatenate([first, cross], 1), jnp.concatenate([cross.T, second], 1)], 0)


def body(bases, gains, scales):
    rank = bases.shape[-1]
    local_rows = bases.shape[1] * bases.shape[2]
    bits_x = lax.axis_size("gx").bit_length() - 1
    bits_y = lax.axis_size("gy").bit_length() - 1
    panels = jnp.concatenate([bases, gains], axis=-1).reshape(LEVELS, local_rows, 2 * rank)
    packed = []
    needs = []
    sizes = []
    for k in range(LEVELS):
        groups = (bits_x - (k + 1) // 2, bits_y - k // 2)
        gram = jnp.dot(panels[k].T, panels[k], preferred_element_type=jnp.float32)
        packed.append(pack(gram, rank))
        needs.append([("gx", bit) for bit in range(groups[0])] + [("gy", bit) for bit in range(groups[1])])
        sizes.append(local_rows * 2 ** (groups[0] + groups[1]))
    gram0 = jnp.stack([unpack(item, rank) for item in node_sums(packed, needs)])
    n_rows = jnp.array(sizes, jnp.float32)[:, None, None]
    root_n = jnp.array([math.sqrt(n) for n in sizes], jnp.float32)[:, None, None]
    weights = scales[:, :, None]
    gram1 = weights * gram0 * tr(weights) / n_rows
    low1, inv1 = chol_inv_blocked(gram1, rank)
    t1 = weights * tr(inv1) / root_n
    q1 = bmm(panels.astype(jnp.float32), t1)
    kernel = bmm(tr(low1), low1)
    first_w = orthonormal(kernel[:, :, :rank])
    second_w = orthonormal(bmm(kernel, first_w))
    core = bmm(bmm(tr(second_w), kernel), second_w)
    basis = (bmm(q1, second_w) * root_n).astype(jnp.bfloat16)
    return (basis.reshape(bases.shape), core.reshape(LEVELS, 1, 1, rank, rank))


def solution(mesh):
    in_specs = (P(None, "gx", "gy", None), P(None, "gx", "gy", None), P())
    out_specs = (P(None, "gx", "gy", None), P(None, "gx", "gy", None, None))
    return jax.shard_map(body, mesh=mesh, in_specs=in_specs, out_specs=out_specs, check_vma=False)
```

```python
import math

import jax
import jax.numpy as jnp
from jax import lax
from jax.experimental import pallas as pl
from jax.sharding import PartitionSpec as P

LEVELS = 3


def exchanged(block, axis, mask):
    count = lax.axis_size(axis)
    route = [(low, low ^ mask) for low in range(count) if low ^ mask < count]
    return lax.ppermute(block, axis, route)


def bmm(left, right):
    return jnp.einsum("bij,bjk->bik", left, right, precision=lax.Precision.HIGHEST)


def tr(block):
    return jnp.swapaxes(block, -1, -2)


def chol_inv_kernel(a_ref, lt_ref, w_ref):
    nb, n, _ = a_ref.shape
    nt = n // 8
    lane = lax.broadcasted_iota(jnp.int32, (1, n), 1)
    sub8 = lax.broadcasted_iota(jnp.int32, (8, 1), 0)
    rows8 = lax.broadcasted_iota(jnp.int32, (8, n), 0)
    cols8 = lax.broadcasted_iota(jnp.int32, (8, n), 1)
    a = [[a_ref[b, 8 * u:8 * u + 8, :] for u in range(nt)] for b in range(nb)]
    w = [[jnp.where(cols8 == rows8 + 8 * u, 1.0, 0.0).astype(jnp.float32) for u in range(nt)] for b in range(nb)]
    lt = [[None] * nt for b in range(nb)]
    for j in range(n):
        u0, s = divmod(j, 8)
        for b in range(nb):
            rowj = a[b][u0][s:s + 1, :]
            r = lax.rsqrt(rowj[:, j:j + 1])
            lrow = jnp.where(lane >= j, rowj * r, 0.0)
            if s == 0:
                lt[b][u0] = jnp.broadcast_to(lrow, (8, n))
            else:
                lt[b][u0] = jnp.where(sub8 == s, lrow, lt[b][u0])
            xrow = w[b][u0][s:s + 1, :] * r
            for u in range(u0, nt):
                col = a[b][u][:, j:j + 1] * r
                if u == u0:
                    col = jnp.where(sub8 >= s, col, 0.0)
                    wcol = col - jnp.where(sub8 == s, 1.0, 0.0)
                else:
                    wcol = col
                a[b][u] = a[b][u] - col * lrow
                w[b][u] = w[b][u] - wcol * xrow
    for b in range(nb):
        for u in range(nt):
            lt_ref[b, 8 * u:8 * u + 8, :] = lt[b][u]
            w_ref[b, 8 * u:8 * u + 8, :] = w[b][u]


def chol_inv(block):
    block = (block + tr(block)) / 2
    shape = jax.ShapeDtypeStruct(block.shape, jnp.float32)
    upper, inverse = pl.pallas_call(chol_inv_kernel, out_shape=(shape, shape))(block)
    return tr(upper), inverse


def chol_inv_blocked(block, half):
    block = (block + tr(block)) / 2
    low11, inv11 = chol_inv(block[:, :half, :half])
    low21 = bmm(block[:, half:, :half], tr(inv11))
    low22, inv22 = chol_inv(block[:, half:, half:] - bmm(low21, tr(low21)))
    inv21 = -bmm(inv22, bmm(low21, inv11))
    zero = jnp.zeros_like(low11)
    low = jnp.concatenate([jnp.concatenate([low11, zero], 2), jnp.concatenate([low21, low22], 2)], 1)
    inverse = jnp.concatenate([jnp.concatenate([inv11, zero], 2), jnp.concatenate([inv21, inv22], 2)], 1)
    return low, inverse


def orthonormal(block):
    _, inverse = chol_inv(bmm(tr(block), block))
    return bmm(block, tr(inverse))


def round_orders(needs):
    best = [list(bits) for bits in needs]

    def search(left, round_no, orders, budget):
        if all(not bits for bits in left):
            return orders
        if budget[0] <= 0:
            return None
        budget[0] -= 1
        active = sorted((i for i in range(len(left)) if left[i]), key=lambda i: -len(left[i]))

        def place(pos, used, picks):
            if pos == len(active):
                new_left = [list(bits) for bits in left]
                new_orders = [list(order) for order in orders]
                for i, bit in picks:
                    new_left[i].remove(bit)
                    new_orders[i].append(bit)
                return search(new_left, round_no + 1, new_orders, budget)
            i = active[pos]
            for bit in left[i]:
                link = bit if bit[0] == "gx" else ("gy",)
                if link not in used:
                    found = place(pos + 1, used | {link}, picks + [(i, bit)])
                    if found:
                        return found
            return None

        return place(0, frozenset(), [])

    found = search([list(bits) for bits in needs], 0, [[] for _ in needs], [2000])
    return found if found else best


def node_sums(items, needs):
    orders = round_orders(needs)
    count_y = lax.axis_size("gy")
    out = []
    for item, order in zip(items, orders):
        masks = [count_y << bit if axis == "gx" else 1 << bit for axis, bit in order]
        for pos in range(0, len(masks), 2):
            if pos + 1 == len(masks):
                item = item + exchanged(item, ("gx", "gy"), masks[pos])
            else:
                first, second = masks[pos], masks[pos + 1]
                near = item + exchanged(item, ("gx", "gy"), first)
                far = exchanged(item, ("gx", "gy"), second) + exchanged(item, ("gx", "gy"), first ^ second)
                item = near + far
        out.append(item)
    return out


def pack(gram, rank):
    rows = lax.broadcasted_iota(jnp.int32, (rank, rank), 0)
    cols = lax.broadcasted_iota(jnp.int32, (rank, rank), 1)
    both = jnp.where(rows <= cols, gram[:rank, :rank], gram[rank:, rank:].T)
    diag = jnp.sum(jnp.where(rows == cols, gram[rank:, rank:], 0.0), axis=0, keepdims=True)
    pad = jnp.zeros((7, rank), gram.dtype)
    return jnp.concatenate([both, gram[:rank, rank:], diag, pad], axis=0)


def unpack(packed, rank):
    rows = lax.broadcasted_iota(jnp.int32, (rank, rank), 0)
    cols = lax.broadcasted_iota(jnp.int32, (rank, rank), 1)
    both = packed[:rank]
    cross = packed[rank:2 * rank]
    diag = packed[2 * rank]
    first = jnp.where(rows <= cols, both, both.T)
    second = jnp.where(rows > cols, both, jnp.where(rows == cols, diag[None, :], both.T))
    return jnp.concatenate([jnp.concatenate([first, cross], 1), jnp.concatenate([cross.T, second], 1)], 0)


def body(bases, gains, scales):
    rank = bases.shape[-1]
    local_rows = bases.shape[1] * bases.shape[2]
    bits_x = lax.axis_size("gx").bit_length() - 1
    bits_y = lax.axis_size("gy").bit_length() - 1
    panels = jnp.concatenate([bases, gains], axis=-1).reshape(LEVELS, local_rows, 2 * rank)
    packed = []
    needs = []
    sizes = []
    for k in range(LEVELS):
        groups = (bits_x - (k + 1) // 2, bits_y - k // 2)
        gram = jnp.dot(panels[k].T, panels[k], preferred_element_type=jnp.float32)
        packed.append(pack(gram, rank))
        needs.append([("gx", bit) for bit in range(groups[0])] + [("gy", bit) for bit in range(groups[1])])
        sizes.append(local_rows * 2 ** (groups[0] + groups[1]))
    gram0 = jnp.stack([unpack(item, rank) for item in node_sums(packed, needs)])
    n_rows = jnp.array(sizes, jnp.float32)[:, None, None]
    root_n = jnp.array([math.sqrt(n) for n in sizes], jnp.float32)[:, None, None]
    weights = scales[:, :, None]
    gram1 = weights * gram0 * tr(weights) / n_rows
    low1, inv1 = chol_inv_blocked(gram1, rank)
    t1 = weights * tr(inv1) / root_n
    q1 = bmm(panels.astype(jnp.float32), t1)
    kernel = bmm(tr(low1), low1)
    first_w = orthonormal(kernel[:, :, :rank])
    second_w = orthonormal(bmm(kernel, first_w))
    core = bmm(bmm(tr(second_w), kernel), second_w)
    basis = (bmm(q1, second_w) * root_n).astype(jnp.bfloat16)
    return (basis.reshape(bases.shape), core.reshape(LEVELS, 1, 1, rank, rank))


def solution(mesh):
    in_specs = (P(None, "gx", "gy", None), P(None, "gx", "gy", None), P())
    out_specs = (P(None, "gx", "gy", None), P(None, "gx", "gy", None, None))
    return jax.shard_map(body, mesh=mesh, in_specs=in_specs, out_specs=out_specs, check_vma=False)
```

```python
import math

import jax
import jax.numpy as jnp
from jax import lax
from jax.experimental import pallas as pl
from jax.sharding import PartitionSpec as P

LEVELS = 3


def swapped(block, axis, apart):
    count = lax.axis_size(axis)
    route = []
    for low in range(count):
        high = low | 1 << apart
        if high != low and high < count:
            route += [(low, high), (high, low)]
    return lax.ppermute(block, axis, route)


def bmm(left, right):
    return jnp.einsum("bij,bjk->bik", left, right, precision=lax.Precision.HIGHEST)


def tr(block):
    return jnp.swapaxes(block, -1, -2)


def chol_inv_kernel(a_ref, lt_ref, w_ref):
    nb, n, _ = a_ref.shape
    nt = n // 8
    lane = lax.broadcasted_iota(jnp.int32, (1, n), 1)
    sub8 = lax.broadcasted_iota(jnp.int32, (8, 1), 0)
    rows8 = lax.broadcasted_iota(jnp.int32, (8, n), 0)
    cols8 = lax.broadcasted_iota(jnp.int32, (8, n), 1)
    a = [[a_ref[b, 8 * u:8 * u + 8, :] for u in range(nt)] for b in range(nb)]
    w = [[jnp.where(cols8 == rows8 + 8 * u, 1.0, 0.0).astype(jnp.float32) for u in range(nt)] for b in range(nb)]
    lt = [[None] * nt for b in range(nb)]
    for j in range(n):
        u0, s = divmod(j, 8)
        for b in range(nb):
            rowj = a[b][u0][s:s + 1, :]
            r = lax.rsqrt(rowj[:, j:j + 1])
            lrow = jnp.where(lane >= j, rowj * r, 0.0)
            if s == 0:
                lt[b][u0] = jnp.broadcast_to(lrow, (8, n))
            else:
                lt[b][u0] = jnp.where(sub8 == s, lrow, lt[b][u0])
            xrow = w[b][u0][s:s + 1, :] * r
            for u in range(u0, nt):
                col = a[b][u][:, j:j + 1] * r
                if u == u0:
                    col = jnp.where(sub8 >= s, col, 0.0)
                    wcol = col - jnp.where(sub8 == s, 1.0, 0.0)
                else:
                    wcol = col
                a[b][u] = a[b][u] - col * lrow
                w[b][u] = w[b][u] - wcol * xrow
    for b in range(nb):
        for u in range(nt):
            lt_ref[b, 8 * u:8 * u + 8, :] = lt[b][u]
            w_ref[b, 8 * u:8 * u + 8, :] = w[b][u]


def chol_inv(block):
    block = (block + tr(block)) / 2
    shape = jax.ShapeDtypeStruct(block.shape, jnp.float32)
    upper, inverse = pl.pallas_call(chol_inv_kernel, out_shape=(shape, shape))(block)
    return tr(upper), inverse


def chol_inv_blocked(block, half):
    block = (block + tr(block)) / 2
    low11, inv11 = chol_inv(block[:, :half, :half])
    low21 = bmm(block[:, half:, :half], tr(inv11))
    low22, inv22 = chol_inv(block[:, half:, half:] - bmm(low21, tr(low21)))
    inv21 = -bmm(inv22, bmm(low21, inv11))
    zero = jnp.zeros_like(low11)
    low = jnp.concatenate([jnp.concatenate([low11, zero], 2), jnp.concatenate([low21, low22], 2)], 1)
    inverse = jnp.concatenate([jnp.concatenate([inv11, zero], 2), jnp.concatenate([inv21, inv22], 2)], 1)
    return low, inverse


def orthonormal(block):
    _, inverse = chol_inv(bmm(tr(block), block))
    return bmm(block, tr(inverse))


def node_sums(stack, needs):
    rounds = sorted({bit for bits in needs for bit in bits}, key=lambda bit: (-sum(bit in bits for bits in needs), bit))
    for axis, bit in rounds:
        users = sum((axis, bit) in bits for bits in needs)
        head = stack[:users]
        head = head + swapped(head, axis, bit)
        stack = head if users == len(needs) else jnp.concatenate([head, stack[users:]], 0)
    return stack


def pack(gram, rank):
    rows = lax.broadcasted_iota(jnp.int32, (rank, rank), 0)
    cols = lax.broadcasted_iota(jnp.int32, (rank, rank), 1)
    both = jnp.where(rows <= cols, gram[:rank, :rank], gram[rank:, rank:].T)
    diag = jnp.sum(jnp.where(rows == cols, gram[rank:, rank:], 0.0), axis=0, keepdims=True)
    pad = jnp.zeros((7, rank), gram.dtype)
    return jnp.concatenate([both, gram[:rank, rank:], diag, pad], axis=0)


def unpack(packed, rank):
    rows = lax.broadcasted_iota(jnp.int32, (rank, rank), 0)
    cols = lax.broadcasted_iota(jnp.int32, (rank, rank), 1)
    both = packed[:rank]
    cross = packed[rank:2 * rank]
    diag = packed[2 * rank]
    first = jnp.where(rows <= cols, both, both.T)
    second = jnp.where(rows > cols, both, jnp.where(rows == cols, diag[None, :], both.T))
    return jnp.concatenate([jnp.concatenate([first, cross], 1), jnp.concatenate([cross.T, second], 1)], 0)


def body(bases, gains, scales):
    rank = bases.shape[-1]
    local_rows = bases.shape[1] * bases.shape[2]
    bits_x = lax.axis_size("gx").bit_length() - 1
    bits_y = lax.axis_size("gy").bit_length() - 1
    panels = jnp.concatenate([bases, gains], axis=-1).reshape(LEVELS, local_rows, 2 * rank)
    packed = []
    needs = []
    sizes = []
    for k in range(LEVELS):
        groups = (bits_x - (k + 1) // 2, bits_y - k // 2)
        gram = jnp.dot(panels[k].T, panels[k], preferred_element_type=jnp.float32)
        packed.append(pack(gram, rank))
        needs.append([("gx", bit) for bit in range(groups[0])] + [("gy", bit) for bit in range(groups[1])])
        sizes.append(local_rows * 2 ** (groups[0] + groups[1]))
    summed = node_sums(jnp.stack(packed), needs)
    gram0 = jnp.stack([unpack(summed[k], rank) for k in range(LEVELS)])
    n_rows = jnp.array(sizes, jnp.float32)[:, None, None]
    root_n = jnp.array([math.sqrt(n) for n in sizes], jnp.float32)[:, None, None]
    weights = scales[:, :, None]
    gram1 = weights * gram0 * tr(weights) / n_rows
    low1, inv1 = chol_inv_blocked(gram1, rank)
    t1 = weights * tr(inv1) / root_n
    q1 = bmm(panels.astype(jnp.float32), t1)
    kernel = bmm(tr(low1), low1)
    first_w = orthonormal(kernel[:, :, :rank])
    second_w = orthonormal(bmm(kernel, first_w))
    core = bmm(bmm(tr(second_w), kernel), second_w)
    basis = (bmm(q1, second_w) * root_n).astype(jnp.bfloat16)
    return (basis.reshape(bases.shape), core.reshape(LEVELS, 1, 1, rank, rank))


def solution(mesh):
    in_specs = (P(None, "gx", "gy", None), P(None, "gx", "gy", None), P())
    out_specs = (P(None, "gx", "gy", None), P(None, "gx", "gy", None, None))
    return jax.shard_map(body, mesh=mesh, in_specs=in_specs, out_specs=out_specs, check_vma=False)
```

```python
import jax
import jax.numpy as jnp
from jax import lax
from jax.experimental import pallas as pl
from jax.sharding import PartitionSpec as P

LEVELS = 3


def swapped(block, axis, apart):
    count = lax.axis_size(axis)
    route = []
    for low in range(count):
        high = low | 1 << apart
        if high != low and high < count:
            route += [(low, high), (high, low)]
    return lax.ppermute(block, axis, route)


def bmm(left, right):
    return jnp.einsum("bij,bjk->bik", left, right, precision=lax.Precision.HIGHEST)


def tr(block):
    return jnp.swapaxes(block, -1, -2)


def chol_inv_kernel(a_ref, lt_ref, w_ref):
    nb, n, _ = a_ref.shape
    nt = n // 8
    lane = lax.broadcasted_iota(jnp.int32, (1, n), 1)
    sub8 = lax.broadcasted_iota(jnp.int32, (8, 1), 0)
    rows8 = lax.broadcasted_iota(jnp.int32, (8, n), 0)
    cols8 = lax.broadcasted_iota(jnp.int32, (8, n), 1)
    a = [[a_ref[b, 8 * u:8 * u + 8, :] for u in range(nt)] for b in range(nb)]
    w = [[jnp.where(cols8 == rows8 + 8 * u, 1.0, 0.0).astype(jnp.float32) for u in range(nt)] for b in range(nb)]
    lt = [[None] * nt for b in range(nb)]
    for j in range(n):
        u0, s = divmod(j, 8)
        for b in range(nb):
            rowj = a[b][u0][s:s + 1, :]
            r = lax.rsqrt(rowj[:, j:j + 1])
            lrow = jnp.where(lane >= j, rowj * r, 0.0)
            if s == 0:
                lt[b][u0] = jnp.broadcast_to(lrow, (8, n))
            else:
                lt[b][u0] = jnp.where(sub8 == s, lrow, lt[b][u0])
            xrow = w[b][u0][s:s + 1, :] * r
            for u in range(u0, nt):
                col = a[b][u][:, j:j + 1] * r
                if u == u0:
                    col = jnp.where(sub8 >= s, col, 0.0)
                    wcol = col - jnp.where(sub8 == s, 1.0, 0.0)
                else:
                    wcol = col
                a[b][u] = a[b][u] - col * lrow
                w[b][u] = w[b][u] - wcol * xrow
    for b in range(nb):
        for u in range(nt):
            lt_ref[b, 8 * u:8 * u + 8, :] = lt[b][u]
            w_ref[b, 8 * u:8 * u + 8, :] = w[b][u]


def chol_inv(block):
    block = (block + tr(block)) / 2
    shape = jax.ShapeDtypeStruct(block.shape, jnp.float32)
    upper, inverse = pl.pallas_call(chol_inv_kernel, out_shape=(shape, shape))(block)
    return tr(upper), inverse


def chol_inv_blocked(block, half):
    block = (block + tr(block)) / 2
    low11, inv11 = chol_inv(block[:, :half, :half])
    low21 = bmm(block[:, half:, :half], tr(inv11))
    low22, inv22 = chol_inv(block[:, half:, half:] - bmm(low21, tr(low21)))
    inv21 = -bmm(inv22, bmm(low21, inv11))
    zero = jnp.zeros_like(low11)
    low = jnp.concatenate([jnp.concatenate([low11, zero], 2), jnp.concatenate([low21, low22], 2)], 1)
    inverse = jnp.concatenate([jnp.concatenate([inv11, zero], 2), jnp.concatenate([inv21, inv22], 2)], 1)
    return low, inverse


def orthonormal(block):
    _, inverse = chol_inv(bmm(tr(block), block))
    return bmm(block, tr(inverse))


def round_orders(needs):
    best = [list(bits) for bits in needs]

    def search(left, round_no, orders, budget):
        if all(not bits for bits in left):
            return orders
        if budget[0] <= 0:
            return None
        budget[0] -= 1
        active = sorted((i for i in range(len(left)) if left[i]), key=lambda i: -len(left[i]))

        def place(pos, used, picks):
            if pos == len(active):
                new_left = [list(bits) for bits in left]
                new_orders = [list(order) for order in orders]
                for i, bit in picks:
                    new_left[i].remove(bit)
                    new_orders[i].append(bit)
                return search(new_left, round_no + 1, new_orders, budget)
            i = active[pos]
            for bit in left[i]:
                link = bit if bit[0] == "gx" else ("gy",)
                if link not in used:
                    found = place(pos + 1, used | {link}, picks + [(i, bit)])
                    if found:
                        return found
            return None

        return place(0, frozenset(), [])

    found = search([list(bits) for bits in needs], 0, [[] for _ in needs], [2000])
    return found if found else best


def node_sums(items, needs):
    orders = round_orders(needs)
    out = []
    for item, order in zip(items, orders):
        for axis, bit in order:
            item = item + swapped(item, axis, bit)
        out.append(item)
    return out


def pack(gram, rank):
    rows = lax.broadcasted_iota(jnp.int32, (rank, rank), 0)
    cols = lax.broadcasted_iota(jnp.int32, (rank, rank), 1)
    both = jnp.where(rows <= cols, gram[:rank, :rank], gram[rank:, rank:].T)
    diag = jnp.sum(jnp.where(rows == cols, gram[rank:, rank:], 0.0), axis=0, keepdims=True)
    pad = jnp.zeros((7, rank), gram.dtype)
    return jnp.concatenate([both, gram[:rank, rank:], diag, pad], axis=0)


def unpack(packed, rank):
    rows = lax.broadcasted_iota(jnp.int32, (rank, rank), 0)
    cols = lax.broadcasted_iota(jnp.int32, (rank, rank), 1)
    both = packed[:rank]
    cross = packed[rank:2 * rank]
    diag = packed[2 * rank]
    first = jnp.where(rows <= cols, both, both.T)
    second = jnp.where(rows > cols, both, jnp.where(rows == cols, diag[None, :], both.T))
    return jnp.concatenate([jnp.concatenate([first, cross], 1), jnp.concatenate([cross.T, second], 1)], 0)


def body(bases, gains, scales):
    rank = bases.shape[-1]
    local_rows = bases.shape[1] * bases.shape[2]
    bits_x = lax.axis_size("gx").bit_length() - 1
    bits_y = lax.axis_size("gy").bit_length() - 1
    panels = jnp.concatenate([bases, gains], axis=-1).reshape(LEVELS, local_rows, 2 * rank)
    packed = []
    needs = []
    sizes = []
    for k in range(LEVELS):
        groups = (bits_x - (k + 1) // 2, bits_y - k // 2)
        gram = jnp.dot(panels[k].T, panels[k], preferred_element_type=jnp.float32)
        packed.append(pack(gram, rank))
        needs.append([("gx", bit) for bit in range(groups[0])] + [("gy", bit) for bit in range(groups[1])])
        sizes.append(local_rows * 2 ** (groups[0] + groups[1]))
    gram0 = jnp.stack([unpack(item, rank) for item in node_sums(packed, needs)])
    n_rows = jnp.array(sizes, jnp.float32)[:, None, None]
    weights = scales[:, :, None]
    gram1 = weights * gram0 * tr(weights) / n_rows
    low1, inv1 = chol_inv_blocked(gram1, rank)
    kernel = bmm(tr(low1), low1)
    first_w = orthonormal(kernel[:, :, :rank])
    second_w = orthonormal(bmm(kernel, first_w))
    core = bmm(bmm(tr(second_w), kernel), second_w)
    mixing = weights * bmm(tr(inv1), second_w)
    basis = jnp.zeros(panels.shape[:2] + (rank,), jnp.float32)
    for _ in range(3):
        part = lax.reduce_precision(mixing, exponent_bits=8, mantissa_bits=7)
        mixing = mixing - part
        basis = basis + jnp.einsum("bij,bjk->bik", panels, part.astype(jnp.bfloat16), preferred_element_type=jnp.float32)
    basis = basis.astype(jnp.bfloat16)
    return (basis.reshape(bases.shape), core.reshape(LEVELS, 1, 1, rank, rank))


def solution(mesh):
    in_specs = (P(None, "gx", "gy", None), P(None, "gx", "gy", None), P())
    out_specs = (P(None, "gx", "gy", None), P(None, "gx", "gy", None, None))
    return jax.shard_map(body, mesh=mesh, in_specs=in_specs, out_specs=out_specs, check_vma=False)
```

```python
import jax
import jax.numpy as jnp
from jax import lax
from jax.experimental import pallas as pl
from jax.experimental.pallas import tpu as pltpu
from jax.sharding import PartitionSpec as P

LEVELS = 3


def swapped(block, axis, apart):
    count = lax.axis_size(axis)
    route = []
    for low in range(count):
        high = low | 1 << apart
        if high != low and high < count:
            route += [(low, high), (high, low)]
    return lax.ppermute(block, axis, route)


def tr(block):
    return jnp.swapaxes(block, -1, -2)


def dot(left, right):
    return jnp.dot(left, right, precision=lax.Precision.HIGHEST, preferred_element_type=jnp.float32)


def sym(block):
    return (block + block.T) / 2


def factor(ain, lt_ref, w_ref):
    nb, n, _ = ain.shape
    nt = n // 8
    lane = lax.broadcasted_iota(jnp.int32, (1, n), 1)
    sub8 = lax.broadcasted_iota(jnp.int32, (8, 1), 0)
    rows8 = lax.broadcasted_iota(jnp.int32, (8, n), 0)
    cols8 = lax.broadcasted_iota(jnp.int32, (8, n), 1)
    a = [[ain[b, 8 * u:8 * u + 8, :] for u in range(nt)] for b in range(nb)]
    w = [[jnp.where(cols8 == rows8 + 8 * u, 1.0, 0.0).astype(jnp.float32) for u in range(nt)] for b in range(nb)]
    lt = [[None] * nt for b in range(nb)]
    for j in range(n):
        u0, s = divmod(j, 8)
        for b in range(nb):
            rowj = a[b][u0][s:s + 1, :]
            r = lax.rsqrt(rowj[:, j:j + 1])
            lrow = jnp.where(lane >= j, rowj * r, 0.0)
            if s == 0:
                lt[b][u0] = jnp.broadcast_to(lrow, (8, n))
            else:
                lt[b][u0] = jnp.where(sub8 == s, lrow, lt[b][u0])
            xrow = w[b][u0][s:s + 1, :] * r
            for u in range(u0, nt):
                col = a[b][u][:, j:j + 1] * r
                if u == u0:
                    col = jnp.where(sub8 >= s, col, 0.0)
                    wcol = col - jnp.where(sub8 == s, 1.0, 0.0)
                else:
                    wcol = col
                a[b][u] = a[b][u] - col * lrow
                w[b][u] = w[b][u] - wcol * xrow
    for b in range(nb):
        for u in range(nt):
            lt_ref[b, 8 * u:8 * u + 8, :] = lt[b][u]
            w_ref[b, 8 * u:8 * u + 8, :] = w[b][u]


def truncate_kernel(g_ref, core_ref, mix_ref, ain, lt, winv, l21, low, inv, kern, zed):
    nb, m, _ = ain.shape

    def stage(step, carry):
        @pl.when(step == 0)
        def _():
            for b in range(nb):
                ain[b] = g_ref[b, :m, :m]

        @pl.when(step == 1)
        def _():
            for b in range(nb):
                inv11 = winv[b]
                low[b, :m, :m] = lt[b].T
                low[b, :m, m:] = jnp.zeros((m, m), jnp.float32)
                inv[b, :m, :m] = inv11
                inv[b, :m, m:] = jnp.zeros((m, m), jnp.float32)
                low21 = dot(g_ref[b, m:, :m], inv11.T)
                l21[b] = low21
                low[b, m:, :m] = low21
                ain[b] = sym(g_ref[b, m:, m:] - dot(low21, low21.T))

        @pl.when(step == 2)
        def _():
            for b in range(nb):
                inv22 = winv[b]
                low[b, m:, m:] = lt[b].T
                inv[b, m:, m:] = inv22
                inv[b, m:, :m] = -dot(inv22, dot(l21[b], inv[b, :m, :m]))
                full = low[b]
                kernel = dot(full.T, full)
                kern[b] = kernel
                first = kernel[:, :m]
                ain[b] = sym(dot(first.T, first))

        @pl.when(step == 3)
        def _():
            for b in range(nb):
                first_w = dot(kern[b, :, :m], winv[b].T)
                zz = dot(kern[b], first_w)
                zed[b] = zz
                ain[b] = sym(dot(zz.T, zz))

        factor(ain, lt, winv)
        return carry

    lax.fori_loop(0, 4, stage, 0)
    for b in range(nb):
        second_w = dot(zed[b], winv[b].T)
        core_ref[b] = dot(dot(second_w.T, kern[b]), second_w)
        mix_ref[b] = dot(inv[b].T, second_w)


def truncate_all(gram1, rank):
    nb, n, _ = gram1.shape
    small = pltpu.VMEM((nb, rank, rank), jnp.float32)
    big = pltpu.VMEM((nb, n, n), jnp.float32)
    return pl.pallas_call(
        truncate_kernel,
        out_shape=(jax.ShapeDtypeStruct((nb, rank, rank), jnp.float32), jax.ShapeDtypeStruct((nb, n, rank), jnp.float32)),
        scratch_shapes=[small, small, small, small, big, big, big, pltpu.VMEM((nb, n, rank), jnp.float32)],
    )(gram1)


def round_orders(needs):
    best = [list(bits) for bits in needs]

    def search(left, round_no, orders, budget):
        if all(not bits for bits in left):
            return orders
        if budget[0] <= 0:
            return None
        budget[0] -= 1
        active = sorted((i for i in range(len(left)) if left[i]), key=lambda i: -len(left[i]))

        def place(pos, used, picks):
            if pos == len(active):
                new_left = [list(bits) for bits in left]
                new_orders = [list(order) for order in orders]
                for i, bit in picks:
                    new_left[i].remove(bit)
                    new_orders[i].append(bit)
                return search(new_left, round_no + 1, new_orders, budget)
            i = active[pos]
            for bit in left[i]:
                link = bit if bit[0] == "gx" else ("gy",)
                if link not in used:
                    found = place(pos + 1, used | {link}, picks + [(i, bit)])
                    if found:
                        return found
            return None

        return place(0, frozenset(), [])

    found = search([list(bits) for bits in needs], 0, [[] for _ in needs], [2000])
    return found if found else best


def node_sums(items, needs):
    orders = round_orders(needs)
    out = []
    for item, order in zip(items, orders):
        for axis, bit in order:
            item = item + swapped(item, axis, bit)
        out.append(item)
    return out


def pack(gram, rank):
    rows = lax.broadcasted_iota(jnp.int32, (rank, rank), 0)
    cols = lax.broadcasted_iota(jnp.int32, (rank, rank), 1)
    both = jnp.where(rows <= cols, gram[:rank, :rank], gram[rank:, rank:].T)
    diag = jnp.sum(jnp.where(rows == cols, gram[rank:, rank:], 0.0), axis=0, keepdims=True)
    pad = jnp.zeros((7, rank), gram.dtype)
    return jnp.concatenate([both, gram[:rank, rank:], diag, pad], axis=0)


def unpack(packed, rank):
    rows = lax.broadcasted_iota(jnp.int32, (rank, rank), 0)
    cols = lax.broadcasted_iota(jnp.int32, (rank, rank), 1)
    both = packed[:rank]
    cross = packed[rank:2 * rank]
    diag = packed[2 * rank]
    first = jnp.where(rows <= cols, both, both.T)
    second = jnp.where(rows > cols, both, jnp.where(rows == cols, diag[None, :], both.T))
    return jnp.concatenate([jnp.concatenate([first, cross], 1), jnp.concatenate([cross.T, second], 1)], 0)


def body(bases, gains, scales):
    rank = bases.shape[-1]
    local_rows = bases.shape[1] * bases.shape[2]
    bits_x = lax.axis_size("gx").bit_length() - 1
    bits_y = lax.axis_size("gy").bit_length() - 1
    panels = jnp.concatenate([bases, gains], axis=-1).reshape(LEVELS, local_rows, 2 * rank)
    packed = []
    needs = []
    sizes = []
    for k in range(LEVELS):
        groups = (bits_x - (k + 1) // 2, bits_y - k // 2)
        gram = jnp.dot(panels[k].T, panels[k], preferred_element_type=jnp.float32)
        packed.append(pack(gram, rank))
        needs.append([("gx", bit) for bit in range(groups[0])] + [("gy", bit) for bit in range(groups[1])])
        sizes.append(local_rows * 2 ** (groups[0] + groups[1]))
    gram0 = jnp.stack([unpack(item, rank) for item in node_sums(packed, needs)])
    n_rows = jnp.array(sizes, jnp.float32)[:, None, None]
    weights = scales[:, :, None]
    gram1 = weights * gram0 * tr(weights) / n_rows
    core, mixing = truncate_all((gram1 + tr(gram1)) / 2, rank)
    mixing = weights * mixing
    basis = jnp.zeros(panels.shape[:2] + (rank,), jnp.float32)
    for _ in range(3):
        part = lax.reduce_precision(mixing, exponent_bits=8, mantissa_bits=7)
        mixing = mixing - part
        basis = basis + jnp.einsum("bij,bjk->bik", panels, part.astype(jnp.bfloat16), preferred_element_type=jnp.float32)
    basis = basis.astype(jnp.bfloat16)
    return (basis.reshape(bases.shape), core.reshape(LEVELS, 1, 1, rank, rank))


def solution(mesh):
    in_specs = (P(None, "gx", "gy", None), P(None, "gx", "gy", None), P())
    out_specs = (P(None, "gx", "gy", None), P(None, "gx", "gy", None, None))
    return jax.shard_map(body, mesh=mesh, in_specs=in_specs, out_specs=out_specs, check_vma=False)
```

```python
import jax
import jax.numpy as jnp
from jax import lax
from jax.experimental import pallas as pl
from jax.experimental.pallas import tpu as pltpu
from jax.sharding import PartitionSpec as P

LEVELS = 3


def swapped(block, axis, apart):
    count = lax.axis_size(axis)
    route = []
    for low in range(count):
        high = low | 1 << apart
        if high != low and high < count:
            route += [(low, high), (high, low)]
    return lax.ppermute(block, axis, route)


def tr(block):
    return jnp.swapaxes(block, -1, -2)


def dot(left, right):
    return jnp.dot(left, right, precision=lax.Precision.HIGHEST, preferred_element_type=jnp.float32)


def sym(block):
    return (block + block.T) / 2


def factor(ain, lt_ref, w_ref):
    nb, n, _ = ain.shape
    nt = n // 8
    lane = lax.broadcasted_iota(jnp.int32, (1, n), 1)
    sub8 = lax.broadcasted_iota(jnp.int32, (8, 1), 0)
    rows8 = lax.broadcasted_iota(jnp.int32, (8, n), 0)
    cols8 = lax.broadcasted_iota(jnp.int32, (8, n), 1)
    a = [[ain[b, 8 * u:8 * u + 8, :] for u in range(nt)] for b in range(nb)]
    w = [[jnp.where(cols8 == rows8 + 8 * u, 1.0, 0.0).astype(jnp.float32) for u in range(nt)] for b in range(nb)]
    lt = [[None] * nt for b in range(nb)]
    for j in range(n):
        u0, s = divmod(j, 8)
        for b in range(nb):
            rowj = a[b][u0][s:s + 1, :]
            r = lax.rsqrt(rowj[:, j:j + 1])
            lrow = jnp.where(lane >= j, rowj * r, 0.0)
            if s == 0:
                lt[b][u0] = jnp.broadcast_to(lrow, (8, n))
            else:
                lt[b][u0] = jnp.where(sub8 == s, lrow, lt[b][u0])
            xrow = w[b][u0][s:s + 1, :] * r
            for u in range(u0, nt):
                col = a[b][u][:, j:j + 1] * r
                if u == u0:
                    col = jnp.where(sub8 >= s, col, 0.0)
                    wcol = col - jnp.where(sub8 == s, 1.0, 0.0)
                else:
                    wcol = col
                a[b][u] = a[b][u] - col * lrow
                w[b][u] = w[b][u] - wcol * xrow
    for b in range(nb):
        for u in range(nt):
            lt_ref[b, 8 * u:8 * u + 8, :] = lt[b][u]
            w_ref[b, 8 * u:8 * u + 8, :] = w[b][u]


def truncate_kernel(g_ref, core_ref, mix_ref, ain, lt, winv, l21, low, inv, kern, zed):
    nb, m, _ = ain.shape

    def stage(step, carry):
        @pl.when(step == 0)
        def _():
            for b in range(nb):
                ain[b] = g_ref[b, :m, :m]

        @pl.when(step == 1)
        def _():
            for b in range(nb):
                inv11 = winv[b]
                low[b, :m, :m] = lt[b].T
                low[b, :m, m:] = jnp.zeros((m, m), jnp.float32)
                inv[b, :m, :m] = inv11
                inv[b, :m, m:] = jnp.zeros((m, m), jnp.float32)
                low21 = dot(g_ref[b, m:, :m], inv11.T)
                l21[b] = low21
                low[b, m:, :m] = low21
                ain[b] = sym(g_ref[b, m:, m:] - dot(low21, low21.T))

        @pl.when(step == 2)
        def _():
            for b in range(nb):
                inv22 = winv[b]
                low[b, m:, m:] = lt[b].T
                inv[b, m:, m:] = inv22
                inv[b, m:, :m] = -dot(inv22, dot(l21[b], inv[b, :m, :m]))
                full = low[b]
                kernel = dot(full.T, full)
                kern[b] = kernel
                first = kernel[:, :m]
                ain[b] = sym(dot(first.T, first))

        @pl.when(step == 3)
        def _():
            for b in range(nb):
                first_w = dot(kern[b, :, :m], winv[b].T)
                zz = dot(kern[b], first_w)
                zed[b] = zz
                ain[b] = sym(dot(zz.T, zz))

        factor(ain, lt, winv)
        return carry

    lax.fori_loop(0, 4, stage, 0)
    for b in range(nb):
        second_w = dot(zed[b], winv[b].T)
        core_ref[b] = dot(dot(second_w.T, kern[b]), second_w)
        mix_ref[b] = dot(inv[b].T, second_w)


def truncate_all(gram1, rank):
    nb, n, _ = gram1.shape
    small = pltpu.VMEM((nb, rank, rank), jnp.float32)
    big = pltpu.VMEM((nb, n, n), jnp.float32)
    return pl.pallas_call(
        truncate_kernel,
        out_shape=(jax.ShapeDtypeStruct((nb, rank, rank), jnp.float32), jax.ShapeDtypeStruct((nb, n, rank), jnp.float32)),
        scratch_shapes=[small, small, small, small, big, big, big, pltpu.VMEM((nb, n, rank), jnp.float32)],
    )(gram1)


def round_orders(needs):
    best = [list(bits) for bits in needs]

    def search(left, round_no, orders, budget):
        if all(not bits for bits in left):
            return orders
        if budget[0] <= 0:
            return None
        budget[0] -= 1
        active = sorted((i for i in range(len(left)) if left[i]), key=lambda i: -len(left[i]))

        def place(pos, used, picks):
            if pos == len(active):
                new_left = [list(bits) for bits in left]
                new_orders = [list(order) for order in orders]
                for i, bit in picks:
                    new_left[i].remove(bit)
                    new_orders[i].append(bit)
                return search(new_left, round_no + 1, new_orders, budget)
            i = active[pos]
            for bit in left[i]:
                link = bit if bit[0] == "gx" else ("gy",)
                if link not in used:
                    found = place(pos + 1, used | {link}, picks + [(i, bit)])
                    if found:
                        return found
            return None

        return place(0, frozenset(), [])

    found = search([list(bits) for bits in needs], 0, [[] for _ in needs], [2000])
    return found if found else best


def node_sums(items, needs):
    orders = round_orders([[bit for bit in bits if bit != ("gx", 0)] for bits in needs])
    core = lax.axis_index("gx") % 2
    half = items[0].shape[0] // 2
    out = []
    for item, order in zip(items, orders):
        low, high = item[:half], item[half:]
        mine = jnp.where(core == 0, low, high)
        mine = mine + swapped(jnp.where(core == 0, high, low), "gx", 0)
        for axis, bit in order:
            mine = mine + swapped(mine, axis, bit)
        other = swapped(mine, "gx", 0)
        out.append(jnp.where(core == 0, jnp.concatenate([mine, other], 0), jnp.concatenate([other, mine], 0)))
    return out


def pack(gram, rank):
    rows = lax.broadcasted_iota(jnp.int32, (rank, rank), 0)
    cols = lax.broadcasted_iota(jnp.int32, (rank, rank), 1)
    both = jnp.where(rows <= cols, gram[:rank, :rank], gram[rank:, rank:].T)
    diag = jnp.sum(jnp.where(rows == cols, gram[rank:, rank:], 0.0), axis=0, keepdims=True)
    pad = jnp.zeros((15, rank), gram.dtype)
    return jnp.concatenate([both, gram[:rank, rank:], diag, pad], axis=0)


def unpack(packed, rank):
    rows = lax.broadcasted_iota(jnp.int32, (rank, rank), 0)
    cols = lax.broadcasted_iota(jnp.int32, (rank, rank), 1)
    both = packed[:rank]
    cross = packed[rank:2 * rank]
    diag = packed[2 * rank]
    first = jnp.where(rows <= cols, both, both.T)
    second = jnp.where(rows > cols, both, jnp.where(rows == cols, diag[None, :], both.T))
    return jnp.concatenate([jnp.concatenate([first, cross], 1), jnp.concatenate([cross.T, second], 1)], 0)


def body(bases, gains, scales):
    rank = bases.shape[-1]
    local_rows = bases.shape[1] * bases.shape[2]
    bits_x = lax.axis_size("gx").bit_length() - 1
    bits_y = lax.axis_size("gy").bit_length() - 1
    panels = jnp.concatenate([bases, gains], axis=-1).reshape(LEVELS, local_rows, 2 * rank)
    packed = []
    needs = []
    sizes = []
    for k in range(LEVELS):
        groups = (bits_x - (k + 1) // 2, bits_y - k // 2)
        gram = jnp.dot(panels[k].T, panels[k], preferred_element_type=jnp.float32)
        packed.append(pack(gram, rank))
        needs.append([("gx", bit) for bit in range(groups[0])] + [("gy", bit) for bit in range(groups[1])])
        sizes.append(local_rows * 2 ** (groups[0] + groups[1]))
    gram0 = jnp.stack([unpack(item, rank) for item in node_sums(packed, needs)])
    n_rows = jnp.array(sizes, jnp.float32)[:, None, None]
    weights = scales[:, :, None]
    gram1 = weights * gram0 * tr(weights) / n_rows
    core, mixing = truncate_all((gram1 + tr(gram1)) / 2, rank)
    mixing = weights * mixing
    basis = jnp.zeros(panels.shape[:2] + (rank,), jnp.float32)
    for _ in range(3):
        part = lax.reduce_precision(mixing, exponent_bits=8, mantissa_bits=7)
        mixing = mixing - part
        basis = basis + jnp.einsum("bij,bjk->bik", panels, part.astype(jnp.bfloat16), preferred_element_type=jnp.float32)
    basis = basis.astype(jnp.bfloat16)
    return (basis.reshape(bases.shape), core.reshape(LEVELS, 1, 1, rank, rank))


def solution(mesh):
    in_specs = (P(None, "gx", "gy", None), P(None, "gx", "gy", None), P())
    out_specs = (P(None, "gx", "gy", None), P(None, "gx", "gy", None, None))
    return jax.shard_map(body, mesh=mesh, in_specs=in_specs, out_specs=out_specs, check_vma=False)
```

```python
import jax
import jax.numpy as jnp
from jax import lax
from jax.experimental import pallas as pl
from jax.experimental.pallas import tpu as pltpu
from jax.sharding import PartitionSpec as P

LEVELS = 3


def swapped(block, axis, apart):
    count = lax.axis_size(axis)
    route = []
    for low in range(count):
        high = low | 1 << apart
        if high != low and high < count:
            route += [(low, high), (high, low)]
    return lax.ppermute(block, axis, route)


def tr(block):
    return jnp.swapaxes(block, -1, -2)


def dot(left, right):
    return jnp.dot(left, right, precision=lax.Precision.HIGHEST, preferred_element_type=jnp.float32)


def sym(block):
    return (block + block.T) / 2


def factor(ain, lt_ref, w_ref):
    nb, n, _ = ain.shape
    nt = n // 8
    lane = lax.broadcasted_iota(jnp.int32, (1, n), 1)
    sub8 = lax.broadcasted_iota(jnp.int32, (8, 1), 0)
    rows8 = lax.broadcasted_iota(jnp.int32, (8, n), 0)
    cols8 = lax.broadcasted_iota(jnp.int32, (8, n), 1)
    a = [[ain[b, 8 * u:8 * u + 8, :] for u in range(nt)] for b in range(nb)]
    w = [[jnp.where(cols8 == rows8 + 8 * u, 1.0, 0.0).astype(jnp.float32) for u in range(nt)] for b in range(nb)]
    lt = [[None] * nt for b in range(nb)]
    for j in range(n):
        u0, s = divmod(j, 8)
        for b in range(nb):
            rowj = a[b][u0][s:s + 1, :]
            r = lax.rsqrt(rowj[:, j:j + 1])
            lrow = jnp.where(lane >= j, rowj * r, 0.0)
            if s == 0:
                lt[b][u0] = jnp.broadcast_to(lrow, (8, n))
            else:
                lt[b][u0] = jnp.where(sub8 == s, lrow, lt[b][u0])
            xrow = w[b][u0][s:s + 1, :] * r
            for u in range(u0, nt):
                col = a[b][u][:, j:j + 1] * r
                if u == u0:
                    col = jnp.where(sub8 >= s, col, 0.0)
                    wcol = col - jnp.where(sub8 == s, 1.0, 0.0)
                else:
                    wcol = col
                a[b][u] = a[b][u] - col * lrow
                w[b][u] = w[b][u] - wcol * xrow
    for b in range(nb):
        for u in range(nt):
            lt_ref[b, 8 * u:8 * u + 8, :] = lt[b][u]
            w_ref[b, 8 * u:8 * u + 8, :] = w[b][u]


def truncate_kernel(g_ref, core_ref, mix_ref, ain, lt, winv, l21, low, inv, kern, zed):
    nb, m, _ = ain.shape

    def stage(step, carry):
        @pl.when(step == 0)
        def _():
            for b in range(nb):
                ain[b] = g_ref[b, :m, :m]

        @pl.when(step == 1)
        def _():
            for b in range(nb):
                inv11 = winv[b]
                low[b, :m, :m] = lt[b].T
                low[b, :m, m:] = jnp.zeros((m, m), jnp.float32)
                inv[b, :m, :m] = inv11
                inv[b, :m, m:] = jnp.zeros((m, m), jnp.float32)
                low21 = dot(g_ref[b, m:, :m], inv11.T)
                l21[b] = low21
                low[b, m:, :m] = low21
                ain[b] = sym(g_ref[b, m:, m:] - dot(low21, low21.T))

        @pl.when(step == 2)
        def _():
            for b in range(nb):
                inv22 = winv[b]
                low[b, m:, m:] = lt[b].T
                inv[b, m:, m:] = inv22
                inv[b, m:, :m] = -dot(inv22, dot(l21[b], inv[b, :m, :m]))
                full = low[b]
                kernel = dot(full.T, full)
                kern[b] = kernel
                first = kernel[:, :m]
                ain[b] = sym(dot(first.T, first))

        @pl.when(step == 3)
        def _():
            for b in range(nb):
                first_w = dot(kern[b, :, :m], winv[b].T)
                zz = dot(kern[b], first_w)
                zed[b] = zz
                ain[b] = sym(dot(zz.T, zz))

        factor(ain, lt, winv)
        return carry

    lax.fori_loop(0, 4, stage, 0)
    for b in range(nb):
        second_w = dot(zed[b], winv[b].T)
        core_ref[b] = dot(dot(second_w.T, kern[b]), second_w)
        mix_ref[b] = dot(inv[b].T, second_w)


def truncate_all(gram1, rank):
    nb, n, _ = gram1.shape
    small = pltpu.VMEM((nb, rank, rank), jnp.float32)
    big = pltpu.VMEM((nb, n, n), jnp.float32)
    return pl.pallas_call(
        truncate_kernel,
        out_shape=(jax.ShapeDtypeStruct((nb, rank, rank), jnp.float32), jax.ShapeDtypeStruct((nb, n, rank), jnp.float32)),
        scratch_shapes=[small, small, small, small, big, big, big, pltpu.VMEM((nb, n, rank), jnp.float32)],
    )(gram1)


def round_orders(needs):
    best = [list(bits) for bits in needs]

    def search(left, round_no, orders, budget):
        if all(not bits for bits in left):
            return orders
        if budget[0] <= 0:
            return None
        budget[0] -= 1
        active = sorted((i for i in range(len(left)) if left[i]), key=lambda i: -len(left[i]))

        def place(pos, used, picks):
            if pos == len(active):
                new_left = [list(bits) for bits in left]
                new_orders = [list(order) for order in orders]
                for i, bit in picks:
                    new_left[i].remove(bit)
                    new_orders[i].append(bit)
                return search(new_left, round_no + 1, new_orders, budget)
            i = active[pos]
            for bit in left[i]:
                link = bit if bit[0] == "gx" else ("gy",)
                if link not in used:
                    found = place(pos + 1, used | {link}, picks + [(i, bit)])
                    if found:
                        return found
            return None

        return place(0, frozenset(), [])

    found = search([list(bits) for bits in needs], 0, [[] for _ in needs], [2000])
    return found if found else best


def node_sums(stack, needs):
    rest = [[bit for bit in bits if bit != ("gx", 0)] for bits in needs]
    rounds = sorted({bit for bits in rest for bit in bits}, key=lambda bit: (-sum(bit in bits for bits in rest), bit))
    core = lax.axis_index("gx") % 2
    half = stack.shape[1] // 2
    low, high = stack[:, :half], stack[:, half:]
    mine = jnp.where(core == 0, low, high) + swapped(jnp.where(core == 0, high, low), "gx", 0)
    for axis, bit in rounds:
        users = sum((axis, bit) in bits for bits in rest)
        head = mine[:users]
        head = head + swapped(head, axis, bit)
        mine = head if users == len(rest) else jnp.concatenate([head, mine[users:]], 0)
    other = swapped(mine, "gx", 0)
    return jnp.where(core == 0, jnp.concatenate([mine, other], 1), jnp.concatenate([other, mine], 1))


def pack(gram, rank):
    rows = lax.broadcasted_iota(jnp.int32, (rank, rank), 0)
    cols = lax.broadcasted_iota(jnp.int32, (rank, rank), 1)
    both = jnp.where(rows <= cols, gram[:rank, :rank], gram[rank:, rank:].T)
    diag = jnp.sum(jnp.where(rows == cols, gram[rank:, rank:], 0.0), axis=0, keepdims=True)
    pad = jnp.zeros((15, rank), gram.dtype)
    return jnp.concatenate([both, gram[:rank, rank:], diag, pad], axis=0)


def unpack(packed, rank):
    rows = lax.broadcasted_iota(jnp.int32, (rank, rank), 0)
    cols = lax.broadcasted_iota(jnp.int32, (rank, rank), 1)
    both = packed[:rank]
    cross = packed[rank:2 * rank]
    diag = packed[2 * rank]
    first = jnp.where(rows <= cols, both, both.T)
    second = jnp.where(rows > cols, both, jnp.where(rows == cols, diag[None, :], both.T))
    return jnp.concatenate([jnp.concatenate([first, cross], 1), jnp.concatenate([cross.T, second], 1)], 0)


def body(bases, gains, scales):
    rank = bases.shape[-1]
    local_rows = bases.shape[1] * bases.shape[2]
    bits_x = lax.axis_size("gx").bit_length() - 1
    bits_y = lax.axis_size("gy").bit_length() - 1
    panels = jnp.concatenate([bases, gains], axis=-1).reshape(LEVELS, local_rows, 2 * rank)
    packed = []
    needs = []
    sizes = []
    for k in range(LEVELS):
        groups = (bits_x - (k + 1) // 2, bits_y - k // 2)
        gram = jnp.dot(panels[k].T, panels[k], preferred_element_type=jnp.float32)
        packed.append(pack(gram, rank))
        needs.append([("gx", bit) for bit in range(groups[0])] + [("gy", bit) for bit in range(groups[1])])
        sizes.append(local_rows * 2 ** (groups[0] + groups[1]))
    summed = node_sums(jnp.stack(packed), needs)
    gram0 = jnp.stack([unpack(summed[k], rank) for k in range(LEVELS)])
    n_rows = jnp.array(sizes, jnp.float32)[:, None, None]
    weights = scales[:, :, None]
    gram1 = weights * gram0 * tr(weights) / n_rows
    core, mixing = truncate_all((gram1 + tr(gram1)) / 2, rank)
    mixing = weights * mixing
    basis = jnp.zeros(panels.shape[:2] + (rank,), jnp.float32)
    for _ in range(3):
        part = lax.reduce_precision(mixing, exponent_bits=8, mantissa_bits=7)
        mixing = mixing - part
        basis = basis + jnp.einsum("bij,bjk->bik", panels, part.astype(jnp.bfloat16), preferred_element_type=jnp.float32)
    basis = basis.astype(jnp.bfloat16)
    return (basis.reshape(bases.shape), core.reshape(LEVELS, 1, 1, rank, rank))


def solution(mesh):
    in_specs = (P(None, "gx", "gy", None), P(None, "gx", "gy", None), P())
    out_specs = (P(None, "gx", "gy", None), P(None, "gx", "gy", None, None))
    return jax.shard_map(body, mesh=mesh, in_specs=in_specs, out_specs=out_specs, check_vma=False)
```

```python
import jax
import jax.numpy as jnp
from jax import lax
from jax.experimental import pallas as pl
from jax.experimental.pallas import tpu as pltpu
from jax.sharding import PartitionSpec as P

LEVELS = 3


def swapped(block, axis, apart):
    count = lax.axis_size(axis)
    route = []
    for low in range(count):
        high = low | 1 << apart
        if high != low and high < count:
            route += [(low, high), (high, low)]
    return lax.ppermute(block, axis, route)


def tr(block):
    return jnp.swapaxes(block, -1, -2)


def dot(left, right):
    return jnp.dot(left, right, precision=lax.Precision.HIGHEST, preferred_element_type=jnp.float32)


def sym(block):
    return (block + block.T) / 2


def factor(ain, lt_ref, w_ref):
    nb, n, _ = ain.shape
    nt = n // 8
    lane = lax.broadcasted_iota(jnp.int32, (1, n), 1)
    sub8 = lax.broadcasted_iota(jnp.int32, (8, 1), 0)
    rows8 = lax.broadcasted_iota(jnp.int32, (8, n), 0)
    cols8 = lax.broadcasted_iota(jnp.int32, (8, n), 1)
    a = [[ain[b, 8 * u:8 * u + 8, :] for u in range(nt)] for b in range(nb)]
    w = [[jnp.where(cols8 == rows8 + 8 * u, 1.0, 0.0).astype(jnp.float32) for u in range(nt)] for b in range(nb)]
    lt = [[None] * nt for b in range(nb)]
    for j in range(n):
        u0, s = divmod(j, 8)
        for b in range(nb):
            rowj = a[b][u0][s:s + 1, :]
            r = lax.rsqrt(rowj[:, j:j + 1])
            lrow = jnp.where(lane >= j, rowj * r, 0.0)
            if s == 0:
                lt[b][u0] = jnp.broadcast_to(lrow, (8, n))
            else:
                lt[b][u0] = jnp.where(sub8 == s, lrow, lt[b][u0])
            xrow = w[b][u0][s:s + 1, :] * r
            for u in range(u0, nt):
                col = a[b][u][:, j:j + 1] * r
                if u == u0:
                    col = jnp.where(sub8 >= s, col, 0.0)
                    wcol = col - jnp.where(sub8 == s, 1.0, 0.0)
                else:
                    wcol = col
                a[b][u] = a[b][u] - col * lrow
                w[b][u] = w[b][u] - wcol * xrow
    for b in range(nb):
        for u in range(nt):
            lt_ref[b, 8 * u:8 * u + 8, :] = lt[b][u]
            w_ref[b, 8 * u:8 * u + 8, :] = w[b][u]


def truncate_kernel(p_ref, s_ref, core_ref, mix_ref, ain, lt, winv, l21, low, inv, kern, zed):
    nb, m, _ = ain.shape
    rows = lax.broadcasted_iota(jnp.int32, (m, m), 0)
    cols = lax.broadcasted_iota(jnp.int32, (m, m), 1)

    def stage(step, carry):
        @pl.when(step == 0)
        def _():
            for b in range(nb):
                both = p_ref[b, :m]
                ain[b] = jnp.where(rows <= cols, both, both.T) * s_ref[b, :m, :m]

        @pl.when(step == 1)
        def _():
            for b in range(nb):
                inv11 = winv[b]
                low[b, :m, :m] = lt[b].T
                low[b, :m, m:] = jnp.zeros((m, m), jnp.float32)
                inv[b, :m, :m] = inv11
                inv[b, :m, m:] = jnp.zeros((m, m), jnp.float32)
                both = p_ref[b, :m]
                lower = jnp.where(rows > cols, both, jnp.where(rows == cols, p_ref[b, 2 * m:2 * m + 1, :], both.T))
                low21 = dot(p_ref[b, m:2 * m].T * s_ref[b, m:, :m], inv11.T)
                l21[b] = low21
                low[b, m:, :m] = low21
                ain[b] = sym(lower * s_ref[b, m:, m:] - dot(low21, low21.T))

        @pl.when(step == 2)
        def _():
            for b in range(nb):
                inv22 = winv[b]
                low[b, m:, m:] = lt[b].T
                inv[b, m:, m:] = inv22
                inv[b, m:, :m] = -dot(inv22, dot(l21[b], inv[b, :m, :m]))
                full = low[b]
                kernel = dot(full.T, full)
                kern[b] = kernel
                first = kernel[:, :m]
                ain[b] = sym(dot(first.T, first))

        @pl.when(step == 3)
        def _():
            for b in range(nb):
                first_w = dot(kern[b, :, :m], winv[b].T)
                zz = dot(kern[b], first_w)
                zed[b] = zz
                ain[b] = sym(dot(zz.T, zz))

        factor(ain, lt, winv)
        return carry

    lax.fori_loop(0, 4, stage, 0)
    for b in range(nb):
        second_w = dot(zed[b], winv[b].T)
        core_ref[b] = dot(dot(second_w.T, kern[b]), second_w)
        mix_ref[b] = dot(inv[b].T, second_w)


def truncate_all(packed, scale, rank):
    nb, n, _ = scale.shape
    small = pltpu.VMEM((nb, rank, rank), jnp.float32)
    big = pltpu.VMEM((nb, n, n), jnp.float32)
    return pl.pallas_call(
        truncate_kernel,
        out_shape=(jax.ShapeDtypeStruct((nb, rank, rank), jnp.float32), jax.ShapeDtypeStruct((nb, n, rank), jnp.float32)),
        scratch_shapes=[small, small, small, small, big, big, big, pltpu.VMEM((nb, n, rank), jnp.float32)],
    )(packed, scale)


def round_orders(needs):
    best = [list(bits) for bits in needs]

    def search(left, round_no, orders, budget):
        if all(not bits for bits in left):
            return orders
        if budget[0] <= 0:
            return None
        budget[0] -= 1
        active = sorted((i for i in range(len(left)) if left[i]), key=lambda i: -len(left[i]))

        def place(pos, used, picks):
            if pos == len(active):
                new_left = [list(bits) for bits in left]
                new_orders = [list(order) for order in orders]
                for i, bit in picks:
                    new_left[i].remove(bit)
                    new_orders[i].append(bit)
                return search(new_left, round_no + 1, new_orders, budget)
            i = active[pos]
            for bit in left[i]:
                link = bit if bit[0] == "gx" else ("gy",)
                if link not in used:
                    found = place(pos + 1, used | {link}, picks + [(i, bit)])
                    if found:
                        return found
            return None

        return place(0, frozenset(), [])

    found = search([list(bits) for bits in needs], 0, [[] for _ in needs], [2000])
    return found if found else best


def node_sums(items, needs):
    orders = round_orders([[bit for bit in bits if bit != ("gx", 0)] for bits in needs])
    core = lax.axis_index("gx") % 2
    half = items[0].shape[0] // 2
    out = []
    for item, order in zip(items, orders):
        low, high = item[:half], item[half:]
        mine = jnp.where(core == 0, low, high)
        mine = mine + swapped(jnp.where(core == 0, high, low), "gx", 0)
        for axis, bit in order:
            mine = mine + swapped(mine, axis, bit)
        other = swapped(mine, "gx", 0)
        out.append(jnp.where(core == 0, jnp.concatenate([mine, other], 0), jnp.concatenate([other, mine], 0)))
    return out


def pack(gram, rank):
    rows = lax.broadcasted_iota(jnp.int32, (rank, rank), 0)
    cols = lax.broadcasted_iota(jnp.int32, (rank, rank), 1)
    both = jnp.where(rows <= cols, gram[0][0], gram[1][1].T)
    diag = jnp.sum(jnp.where(rows == cols, gram[1][1], 0.0), axis=0, keepdims=True)
    pad = jnp.zeros((15, rank), jnp.float32)
    return jnp.concatenate([both, gram[0][1], diag, pad], axis=0)


def body(bases, gains, scales):
    rank = bases.shape[-1]
    local_rows = bases.shape[1] * bases.shape[2]
    bits_x = lax.axis_size("gx").bit_length() - 1
    bits_y = lax.axis_size("gy").bit_length() - 1
    left = bases.reshape(LEVELS, local_rows, rank)
    right = gains.reshape(LEVELS, local_rows, rank)
    packed = []
    needs = []
    sizes = []
    for k in range(LEVELS):
        groups = (bits_x - (k + 1) // 2, bits_y - k // 2)
        gram = [[jnp.dot(one.T, two, preferred_element_type=jnp.float32) for two in (left[k], right[k])] for one in (left[k], right[k])]
        packed.append(pack(gram, rank))
        needs.append([("gx", bit) for bit in range(groups[0])] + [("gy", bit) for bit in range(groups[1])])
        sizes.append(local_rows * 2 ** (groups[0] + groups[1]))
    summed = jnp.stack(node_sums(packed, needs))
    n_rows = jnp.array(sizes, jnp.float32)[:, None, None]
    weights = scales[:, :, None]
    core, mixing = truncate_all(summed, weights * tr(weights) / n_rows, rank)
    mixing = weights * mixing
    basis = jnp.zeros(left.shape, jnp.float32)
    for _ in range(3):
        part = lax.reduce_precision(mixing, exponent_bits=8, mantissa_bits=7)
        mixing = mixing - part
        part = part.astype(jnp.bfloat16)
        basis = basis + jnp.einsum("bij,bjk->bik", left, part[:, :rank], preferred_element_type=jnp.float32)
        basis = basis + jnp.einsum("bij,bjk->bik", right, part[:, rank:], preferred_element_type=jnp.float32)
    basis = basis.astype(jnp.bfloat16)
    return (basis.reshape(bases.shape), core.reshape(LEVELS, 1, 1, rank, rank))


def solution(mesh):
    in_specs = (P(None, "gx", "gy", None), P(None, "gx", "gy", None), P())
    out_specs = (P(None, "gx", "gy", None), P(None, "gx", "gy", None, None))
    return jax.shard_map(body, mesh=mesh, in_specs=in_specs, out_specs=out_specs, check_vma=False)
```

```python
import jax
import jax.numpy as jnp
from jax import lax
from jax.experimental import pallas as pl
from jax.experimental.pallas import tpu as pltpu
from jax.sharding import PartitionSpec as P

LEVELS = 3


def swapped(block, axis, apart):
    count = lax.axis_size(axis)
    route = []
    for low in range(count):
        high = low | 1 << apart
        if high != low and high < count:
            route += [(low, high), (high, low)]
    return lax.ppermute(block, axis, route)


def tr(block):
    return jnp.swapaxes(block, -1, -2)


def dot(left, right):
    return jnp.dot(left, right, precision=lax.Precision.HIGHEST, preferred_element_type=jnp.float32)


def sym(block):
    return (block + block.T) / 2


def factor(ain, lt_ref, w_ref):
    nb, n, _ = ain.shape
    nt = n // 8
    lane = lax.broadcasted_iota(jnp.int32, (1, n), 1)
    sub8 = lax.broadcasted_iota(jnp.int32, (8, 1), 0)
    rows8 = lax.broadcasted_iota(jnp.int32, (8, n), 0)
    cols8 = lax.broadcasted_iota(jnp.int32, (8, n), 1)
    a = [[ain[b, 8 * u:8 * u + 8, :] for u in range(nt)] for b in range(nb)]
    w = [[jnp.where(cols8 == rows8 + 8 * u, 1.0, 0.0).astype(jnp.float32) for u in range(nt)] for b in range(nb)]
    lt = [[None] * nt for b in range(nb)]
    for j in range(n):
        u0, s = divmod(j, 8)
        for b in range(nb):
            rowj = a[b][u0][s:s + 1, :]
            r = lax.rsqrt(rowj[:, j:j + 1])
            lrow = jnp.where(lane >= j, rowj * r, 0.0)
            if s == 0:
                lt[b][u0] = jnp.broadcast_to(lrow, (8, n))
            else:
                lt[b][u0] = jnp.where(sub8 == s, lrow, lt[b][u0])
            xrow = w[b][u0][s:s + 1, :] * r
            for u in range(u0, nt):
                col = a[b][u][:, j:j + 1] * r
                if u == u0:
                    col = jnp.where(sub8 >= s, col, 0.0)
                    wcol = col - jnp.where(sub8 == s, 1.0, 0.0)
                else:
                    wcol = col
                a[b][u] = a[b][u] - col * lrow
                w[b][u] = w[b][u] - wcol * xrow
    for b in range(nb):
        for u in range(nt):
            lt_ref[b, 8 * u:8 * u + 8, :] = lt[b][u]
            w_ref[b, 8 * u:8 * u + 8, :] = w[b][u]


def truncate_kernel(p_ref, s_ref, w_ref, b_hbm, g_hbm, core_ref, out_ref, ain, lt, winv, l21, low, inv, kern, zed,
                    b_vmem, g_vmem, sems):
    nb, m, _ = ain.shape
    rows = lax.broadcasted_iota(jnp.int32, (m, m), 0)
    cols = lax.broadcasted_iota(jnp.int32, (m, m), 1)
    copies = [pltpu.make_async_copy(b_hbm, b_vmem, sems.at[0]), pltpu.make_async_copy(g_hbm, g_vmem, sems.at[1])]
    for copy in copies:
        copy.start()

    def stage(step, carry):
        @pl.when(step == 0)
        def _():
            for b in range(nb):
                both = p_ref[b, :m]
                ain[b] = jnp.where(rows <= cols, both, both.T) * s_ref[b, :m, :m]

        @pl.when(step == 1)
        def _():
            for b in range(nb):
                inv11 = winv[b]
                low[b, :m, :m] = lt[b].T
                low[b, :m, m:] = jnp.zeros((m, m), jnp.float32)
                inv[b, :m, :m] = inv11
                inv[b, :m, m:] = jnp.zeros((m, m), jnp.float32)
                both = p_ref[b, :m]
                lower = jnp.where(rows > cols, both, jnp.where(rows == cols, p_ref[b, 2 * m:2 * m + 1, :], both.T))
                low21 = dot(p_ref[b, m:2 * m].T * s_ref[b, m:, :m], inv11.T)
                l21[b] = low21
                low[b, m:, :m] = low21
                ain[b] = sym(lower * s_ref[b, m:, m:] - dot(low21, low21.T))

        @pl.when(step == 2)
        def _():
            for b in range(nb):
                inv22 = winv[b]
                low[b, m:, m:] = lt[b].T
                inv[b, m:, m:] = inv22
                inv[b, m:, :m] = -dot(inv22, dot(l21[b], inv[b, :m, :m]))
                full = low[b]
                kernel = dot(full.T, full)
                kern[b] = kernel
                first = kernel[:, :m]
                ain[b] = sym(dot(first.T, first))

        @pl.when(step == 3)
        def _():
            for b in range(nb):
                first_w = dot(kern[b, :, :m], winv[b].T)
                zz = dot(kern[b], first_w)
                zed[b] = zz
                ain[b] = sym(dot(zz.T, zz))

        factor(ain, lt, winv)
        return carry

    lax.fori_loop(0, 4, stage, 0)
    for copy in copies:
        copy.wait()
    for b in range(nb):
        second_w = dot(zed[b], winv[b].T)
        core_ref[b] = dot(dot(second_w.T, kern[b]), second_w)
        mixing = w_ref[b] * dot(inv[b].T, second_w)
        basis = jnp.zeros(out_ref.shape[1:], jnp.float32)
        for _ in range(3):
            part = mixing.astype(jnp.bfloat16)
            mixing = mixing - part.astype(jnp.float32)
            basis = basis + jnp.dot(b_vmem[b], part[:m], preferred_element_type=jnp.float32)
            basis = basis + jnp.dot(g_vmem[b], part[m:], preferred_element_type=jnp.float32)
        out_ref[b] = basis.astype(out_ref.dtype)


def truncate_all(packed, scale, weights, left, right, rank):
    nb, n, _ = scale.shape
    small = pltpu.VMEM((nb, rank, rank), jnp.float32)
    big = pltpu.VMEM((nb, n, n), jnp.float32)
    vmem = pl.BlockSpec(memory_space=pltpu.VMEM)
    hbm = pl.BlockSpec(memory_space=pl.ANY)
    return pl.pallas_call(
        truncate_kernel,
        out_shape=(jax.ShapeDtypeStruct((nb, rank, rank), jnp.float32), jax.ShapeDtypeStruct(left.shape, left.dtype)),
        in_specs=[vmem, vmem, vmem, hbm, hbm],
        out_specs=(vmem, vmem),
        scratch_shapes=[small, small, small, small, big, big, big, pltpu.VMEM((nb, n, rank), jnp.float32),
                        pltpu.VMEM(left.shape, left.dtype), pltpu.VMEM(right.shape, right.dtype),
                        pltpu.SemaphoreType.DMA((2,))],
    )(packed, scale, weights, left, right)


def round_orders(needs):
    best = [list(bits) for bits in needs]

    def search(left, round_no, orders, budget):
        if all(not bits for bits in left):
            return orders
        if budget[0] <= 0:
            return None
        budget[0] -= 1
        active = sorted((i for i in range(len(left)) if left[i]), key=lambda i: -len(left[i]))

        def place(pos, used, picks):
            if pos == len(active):
                new_left = [list(bits) for bits in left]
                new_orders = [list(order) for order in orders]
                for i, bit in picks:
                    new_left[i].remove(bit)
                    new_orders[i].append(bit)
                return search(new_left, round_no + 1, new_orders, budget)
            i = active[pos]
            for bit in left[i]:
                link = bit if bit[0] == "gx" else ("gy",)
                if link not in used:
                    found = place(pos + 1, used | {link}, picks + [(i, bit)])
                    if found:
                        return found
            return None

        return place(0, frozenset(), [])

    found = search([list(bits) for bits in needs], 0, [[] for _ in needs], [2000])
    return found if found else best


def node_sums(items, needs):
    orders = round_orders([[bit for bit in bits if bit != ("gx", 0)] for bits in needs])
    core = lax.axis_index("gx") % 2
    half = items[0].shape[0] // 2
    out = []
    for item, order in zip(items, orders):
        low, high = item[:half], item[half:]
        mine = jnp.where(core == 0, low, high)
        mine = mine + swapped(jnp.where(core == 0, high, low), "gx", 0)
        for axis, bit in order:
            mine = mine + swapped(mine, axis, bit)
        other = swapped(mine, "gx", 0)
        out.append(jnp.where(core == 0, jnp.concatenate([mine, other], 0), jnp.concatenate([other, mine], 0)))
    return out


def pack(gram, rank):
    rows = lax.broadcasted_iota(jnp.int32, (rank, rank), 0)
    cols = lax.broadcasted_iota(jnp.int32, (rank, rank), 1)
    both = jnp.where(rows <= cols, gram[0][0], gram[1][1].T)
    diag = jnp.sum(jnp.where(rows == cols, gram[1][1], 0.0), axis=0, keepdims=True)
    pad = jnp.zeros((15, rank), jnp.float32)
    return jnp.concatenate([both, gram[0][1], diag, pad], axis=0)


def body(bases, gains, scales):
    rank = bases.shape[-1]
    local_rows = bases.shape[1] * bases.shape[2]
    bits_x = lax.axis_size("gx").bit_length() - 1
    bits_y = lax.axis_size("gy").bit_length() - 1
    left = bases.reshape(LEVELS, local_rows, rank)
    right = gains.reshape(LEVELS, local_rows, rank)
    packed = []
    needs = []
    sizes = []
    for k in range(LEVELS):
        groups = (bits_x - (k + 1) // 2, bits_y - k // 2)
        gram = [[jnp.dot(one.T, two, preferred_element_type=jnp.float32) for two in (left[k], right[k])] for one in (left[k], right[k])]
        packed.append(pack(gram, rank))
        needs.append([("gx", bit) for bit in range(groups[0])] + [("gy", bit) for bit in range(groups[1])])
        sizes.append(local_rows * 2 ** (groups[0] + groups[1]))
    summed = jnp.stack(node_sums(packed, needs))
    n_rows = jnp.array(sizes, jnp.float32)[:, None, None]
    weights = scales[:, :, None]
    core, basis = truncate_all(summed, weights * tr(weights) / n_rows, jnp.broadcast_to(weights, (LEVELS, 2 * rank, rank)),
                               left, right, rank)
    return (basis.reshape(bases.shape), core.reshape(LEVELS, 1, 1, rank, rank))


def solution(mesh):
    in_specs = (P(None, "gx", "gy", None), P(None, "gx", "gy", None), P())
    out_specs = (P(None, "gx", "gy", None), P(None, "gx", "gy", None, None))
    return jax.shard_map(body, mesh=mesh, in_specs=in_specs, out_specs=out_specs, check_vma=False)
```

```python
import jax
import jax.numpy as jnp
from jax import lax
from jax.experimental import pallas as pl
from jax.experimental.pallas import tpu as pltpu
from jax.sharding import PartitionSpec as P

LEVELS = 3


def swapped(block, axis, apart):
    count = lax.axis_size(axis)
    route = []
    for low in range(count):
        high = low | 1 << apart
        if high != low and high < count:
            route += [(low, high), (high, low)]
    return lax.ppermute(block, axis, route)


def tr(block):
    return jnp.swapaxes(block, -1, -2)


def dot(left, right):
    return jnp.dot(left, right, precision=lax.Precision.HIGHEST, preferred_element_type=jnp.float32)


def sym(block):
    return (block + block.T) / 2


def factor(ain, lt_ref, w_ref):
    nb, n, _ = ain.shape
    nt = n // 8
    rows8 = lax.broadcasted_iota(jnp.int32, (8, n), 0)
    cols8 = lax.broadcasted_iota(jnp.int32, (8, n), 1)
    a = [[ain[b, 8 * u:8 * u + 8, :] for u in range(nt)] for b in range(nb)]
    w = [[jnp.where(cols8 == rows8 + 8 * u, 1.0, 0.0).astype(jnp.float32) for u in range(nt)] for b in range(nb)]
    lt = [[None] * nt for b in range(nb)]
    for j in range(n):
        u0, s = divmod(j, 8)
        for b in range(nb):
            tile = a[b][u0]
            column = jnp.broadcast_to(tile[:, j:j + 1], (8, n))
            r = lax.rsqrt(jnp.broadcast_to(column[s:s + 1, :], (8, n)))
            lrow = jnp.where(cols8 >= j, jnp.broadcast_to(tile[s:s + 1, :], (8, n)) * r, 0.0)
            lt[b][u0] = lrow if s == 0 else jnp.where(rows8 == s, lrow, lt[b][u0])
            xrow = jnp.broadcast_to(w[b][u0][s:s + 1, :], (8, n)) * r
            for u in range(u0, nt):
                if u == u0:
                    col = jnp.where(rows8 >= s, column * r, 0.0)
                    wcol = col - jnp.where(rows8 == s, 1.0, 0.0)
                else:
                    col = jnp.broadcast_to(a[b][u][:, j:j + 1], (8, n)) * r
                    wcol = col
                a[b][u] = a[b][u] - col * lrow
                w[b][u] = w[b][u] - wcol * xrow
    for b in range(nb):
        for u in range(nt):
            lt_ref[b, 8 * u:8 * u + 8, :] = lt[b][u]
            w_ref[b, 8 * u:8 * u + 8, :] = w[b][u]


def truncate_kernel(p_ref, s_ref, w_ref, b_hbm, g_hbm, core_ref, out_ref, ain, lt, winv, l21, low, inv, kern, zed,
                    b_vmem, g_vmem, sems):
    nb, m, _ = ain.shape
    rows = lax.broadcasted_iota(jnp.int32, (m, m), 0)
    cols = lax.broadcasted_iota(jnp.int32, (m, m), 1)
    copies = [pltpu.make_async_copy(b_hbm, b_vmem, sems.at[0]), pltpu.make_async_copy(g_hbm, g_vmem, sems.at[1])]
    for copy in copies:
        copy.start()

    def stage(step, carry):
        @pl.when(step == 0)
        def _():
            for b in range(nb):
                both = p_ref[b, :m]
                ain[b] = jnp.where(rows <= cols, both, both.T) * s_ref[b, :m, :m]

        @pl.when(step == 1)
        def _():
            for b in range(nb):
                inv11 = winv[b]
                low[b, :m, :m] = lt[b].T
                low[b, :m, m:] = jnp.zeros((m, m), jnp.float32)
                inv[b, :m, :m] = inv11
                inv[b, :m, m:] = jnp.zeros((m, m), jnp.float32)
                both = p_ref[b, :m]
                lower = jnp.where(rows > cols, both, jnp.where(rows == cols, p_ref[b, 2 * m:2 * m + 1, :], both.T))
                low21 = dot(p_ref[b, m:2 * m].T * s_ref[b, m:, :m], inv11.T)
                l21[b] = low21
                low[b, m:, :m] = low21
                ain[b] = sym(lower * s_ref[b, m:, m:] - dot(low21, low21.T))

        @pl.when(step == 2)
        def _():
            for b in range(nb):
                inv22 = winv[b]
                low[b, m:, m:] = lt[b].T
                inv[b, m:, m:] = inv22
                inv[b, m:, :m] = -dot(inv22, dot(l21[b], inv[b, :m, :m]))
                full = low[b]
                kernel = dot(full.T, full)
                kern[b] = kernel
                first = kernel[:, :m]
                ain[b] = sym(dot(first.T, first))

        @pl.when(step == 3)
        def _():
            for b in range(nb):
                first_w = dot(kern[b, :, :m], winv[b].T)
                zz = dot(kern[b], first_w)
                zed[b] = zz
                ain[b] = sym(dot(zz.T, zz))

        factor(ain, lt, winv)
        return carry

    lax.fori_loop(0, 4, stage, 0)
    for copy in copies:
        copy.wait()
    for b in range(nb):
        second_w = dot(zed[b], winv[b].T)
        core_ref[b] = dot(dot(second_w.T, kern[b]), second_w)
        mixing = w_ref[b] * dot(inv[b].T, second_w)
        basis = jnp.zeros(out_ref.shape[1:], jnp.float32)
        for _ in range(3):
            part = mixing.astype(jnp.bfloat16)
            mixing = mixing - part.astype(jnp.float32)
            basis = basis + jnp.dot(b_vmem[b], part[:m], preferred_element_type=jnp.float32)
            basis = basis + jnp.dot(g_vmem[b], part[m:], preferred_element_type=jnp.float32)
        out_ref[b] = basis.astype(out_ref.dtype)


def truncate_all(packed, scale, weights, left, right, rank):
    nb, n, _ = scale.shape
    small = pltpu.VMEM((nb, rank, rank), jnp.float32)
    big = pltpu.VMEM((nb, n, n), jnp.float32)
    vmem = pl.BlockSpec(memory_space=pltpu.VMEM)
    hbm = pl.BlockSpec(memory_space=pl.ANY)
    return pl.pallas_call(
        truncate_kernel,
        out_shape=(jax.ShapeDtypeStruct((nb, rank, rank), jnp.float32), jax.ShapeDtypeStruct(left.shape, left.dtype)),
        in_specs=[vmem, vmem, vmem, hbm, hbm],
        out_specs=(vmem, vmem),
        scratch_shapes=[small, small, small, small, big, big, big, pltpu.VMEM((nb, n, rank), jnp.float32),
                        pltpu.VMEM(left.shape, left.dtype), pltpu.VMEM(right.shape, right.dtype),
                        pltpu.SemaphoreType.DMA((2,))],
    )(packed, scale, weights, left, right)


def round_orders(needs):
    best = [list(bits) for bits in needs]

    def search(left, round_no, orders, budget):
        if all(not bits for bits in left):
            return orders
        if budget[0] <= 0:
            return None
        budget[0] -= 1
        active = sorted((i for i in range(len(left)) if left[i]), key=lambda i: -len(left[i]))

        def place(pos, used, picks):
            if pos == len(active):
                new_left = [list(bits) for bits in left]
                new_orders = [list(order) for order in orders]
                for i, bit in picks:
                    new_left[i].remove(bit)
                    new_orders[i].append(bit)
                return search(new_left, round_no + 1, new_orders, budget)
            i = active[pos]
            for bit in left[i]:
                link = bit if bit[0] == "gx" else ("gy",)
                if link not in used:
                    found = place(pos + 1, used | {link}, picks + [(i, bit)])
                    if found:
                        return found
            return None

        return place(0, frozenset(), [])

    found = search([list(bits) for bits in needs], 0, [[] for _ in needs], [2000])
    return found if found else best


def node_sums(items, needs):
    orders = round_orders([[bit for bit in bits if bit != ("gx", 0)] for bits in needs])
    core = lax.axis_index("gx") % 2
    half = items[0].shape[0] // 2
    out = []
    for item, order in zip(items, orders):
        low, high = item[:half], item[half:]
        mine = jnp.where(core == 0, low, high)
        mine = mine + swapped(jnp.where(core == 0, high, low), "gx", 0)
        for axis, bit in order:
            mine = mine + swapped(mine, axis, bit)
        other = swapped(mine, "gx", 0)
        out.append(jnp.where(core == 0, jnp.concatenate([mine, other], 0), jnp.concatenate([other, mine], 0)))
    return out


def pack(gram, rank):
    rows = lax.broadcasted_iota(jnp.int32, (rank, rank), 0)
    cols = lax.broadcasted_iota(jnp.int32, (rank, rank), 1)
    both = jnp.where(rows <= cols, gram[0][0], gram[1][1].T)
    diag = jnp.sum(jnp.where(rows == cols, gram[1][1], 0.0), axis=0, keepdims=True)
    pad = jnp.zeros((15, rank), jnp.float32)
    return jnp.concatenate([both, gram[0][1], diag, pad], axis=0)


def body(bases, gains, scales):
    rank = bases.shape[-1]
    local_rows = bases.shape[1] * bases.shape[2]
    bits_x = lax.axis_size("gx").bit_length() - 1
    bits_y = lax.axis_size("gy").bit_length() - 1
    left = bases.reshape(LEVELS, local_rows, rank)
    right = gains.reshape(LEVELS, local_rows, rank)
    packed = []
    needs = []
    sizes = []
    for k in range(LEVELS):
        groups = (bits_x - (k + 1) // 2, bits_y - k // 2)
        gram = [[jnp.dot(one.T, two, preferred_element_type=jnp.float32) for two in (left[k], right[k])] for one in (left[k], right[k])]
        packed.append(pack(gram, rank))
        needs.append([("gx", bit) for bit in range(groups[0])] + [("gy", bit) for bit in range(groups[1])])
        sizes.append(local_rows * 2 ** (groups[0] + groups[1]))
    summed = jnp.stack(node_sums(packed, needs))
    n_rows = jnp.array(sizes, jnp.float32)[:, None, None]
    weights = scales[:, :, None]
    core, basis = truncate_all(summed, weights * tr(weights) / n_rows, jnp.broadcast_to(weights, (LEVELS, 2 * rank, rank)),
                               left, right, rank)
    return (basis.reshape(bases.shape), core.reshape(LEVELS, 1, 1, rank, rank))


def solution(mesh):
    in_specs = (P(None, "gx", "gy", None), P(None, "gx", "gy", None), P())
    out_specs = (P(None, "gx", "gy", None), P(None, "gx", "gy", None, None))
    return jax.shard_map(body, mesh=mesh, in_specs=in_specs, out_specs=out_specs, check_vma=False)
```

```python
import jax
import jax.numpy as jnp
from jax import lax
from jax.experimental import pallas as pl
from jax.experimental.pallas import tpu as pltpu
from jax.sharding import PartitionSpec as P

LEVELS = 3


def swapped(block, axis, apart):
    count = lax.axis_size(axis)
    route = []
    for low in range(count):
        high = low | 1 << apart
        if high != low and high < count:
            route += [(low, high), (high, low)]
    return lax.ppermute(block, axis, route)


def tr(block):
    return jnp.swapaxes(block, -1, -2)


def dot(left, right):
    return jnp.dot(left, right, precision=lax.Precision.HIGHEST, preferred_element_type=jnp.float32)


def sym(block):
    return (block + block.T) / 2


def factor(ain, lt_ref, w_ref):
    nb, n, _ = ain.shape
    nt = n // 8
    lane = lax.broadcasted_iota(jnp.int32, (1, n), 1)
    sub8 = lax.broadcasted_iota(jnp.int32, (8, 1), 0)
    rows8 = lax.broadcasted_iota(jnp.int32, (8, n), 0)
    cols8 = lax.broadcasted_iota(jnp.int32, (8, n), 1)
    a = [[ain[b, 8 * u:8 * u + 8, :] for u in range(nt)] for b in range(nb)]
    w = [[jnp.where(cols8 == rows8 + 8 * u, 1.0, 0.0).astype(jnp.float32) for u in range(nt)] for b in range(nb)]
    lt = [[None] * nt for b in range(nb)]
    for j in range(n):
        u0, s = divmod(j, 8)
        for b in range(nb):
            rowj = a[b][u0][s:s + 1, :]
            r = lax.rsqrt(rowj[:, j:j + 1])
            lrow = jnp.where(lane >= j, rowj * r, 0.0)
            if s == 0:
                lt[b][u0] = jnp.broadcast_to(lrow, (8, n))
            else:
                lt[b][u0] = jnp.where(sub8 == s, lrow, lt[b][u0])
            xrow = w[b][u0][s:s + 1, :] * r
            for u in range(u0, nt):
                col = a[b][u][:, j:j + 1] * r
                if u == u0:
                    col = jnp.where(sub8 >= s, col, 0.0)
                    wcol = col - jnp.where(sub8 == s, 1.0, 0.0)
                else:
                    wcol = col
                a[b][u] = a[b][u] - col * lrow
                w[b][u] = w[b][u] - wcol * xrow
    for b in range(nb):
        for u in range(nt):
            lt_ref[b, 8 * u:8 * u + 8, :] = lt[b][u]
            w_ref[b, 8 * u:8 * u + 8, :] = w[b][u]


def truncate_kernel(p_ref, s_ref, w_ref, b_hbm, g_hbm, core_ref, out_ref, ain, lt, winv, l21, low, inv, kern, zed,
                    b_vmem, g_vmem, sems):
    nb, m, _ = ain.shape
    rows = lax.broadcasted_iota(jnp.int32, (m, m), 0)
    cols = lax.broadcasted_iota(jnp.int32, (m, m), 1)
    copies = [pltpu.make_async_copy(b_hbm, b_vmem, sems.at[0]), pltpu.make_async_copy(g_hbm, g_vmem, sems.at[1])]
    for copy in copies:
        copy.start()

    def stage(step, carry):
        @pl.when(step == 0)
        def _():
            for b in range(nb):
                both = p_ref[b, :m]
                ain[b] = jnp.where(rows <= cols, both, both.T) * s_ref[b, :m, :m]

        @pl.when(step == 1)
        def _():
            for b in range(nb):
                inv11 = winv[b]
                low[b, :m, :m] = lt[b].T
                low[b, :m, m:] = jnp.zeros((m, m), jnp.float32)
                inv[b, :m, :m] = inv11
                inv[b, :m, m:] = jnp.zeros((m, m), jnp.float32)
                both = p_ref[b, :m]
                lower = jnp.where(rows > cols, both, jnp.where(rows == cols, p_ref[b, 2 * m:2 * m + 1, :], both.T))
                low21 = dot(p_ref[b, m:2 * m].T * s_ref[b, m:, :m], inv11.T)
                l21[b] = low21
                low[b, m:, :m] = low21
                ain[b] = sym(lower * s_ref[b, m:, m:] - dot(low21, low21.T))

        @pl.when(step == 2)
        def _():
            for b in range(nb):
                inv22 = winv[b]
                low[b, m:, m:] = lt[b].T
                inv[b, m:, m:] = inv22
                inv[b, m:, :m] = -dot(inv22, dot(l21[b], inv[b, :m, :m]))
                full = low[b]
                kernel = dot(full.T, full)
                kern[b] = kernel
                first = kernel[:, :m]
                ain[b] = sym(dot(first.T, first))

        @pl.when(step == 3)
        def _():
            for b in range(nb):
                first_w = dot(kern[b, :, :m], winv[b].T)
                zz = dot(kern[b], first_w)
                zed[b] = zz
                ain[b] = sym(dot(zz.T, zz))

        factor(ain, lt, winv)
        return carry

    lax.fori_loop(0, 4, stage, 0)
    for copy in copies:
        copy.wait()
    for b in range(nb):
        second_w = dot(zed[b], winv[b].T)
        core_ref[b] = dot(dot(second_w.T, kern[b]), second_w)
        mixing = dot((inv[b] * w_ref[b]).T, second_w)
        basis = jnp.zeros(out_ref.shape[1:], jnp.float32)
        for _ in range(3):
            part = mixing.astype(jnp.bfloat16)
            mixing = mixing - part.astype(jnp.float32)
            basis = basis + jnp.dot(b_vmem[b], part[:m], preferred_element_type=jnp.float32)
            basis = basis + jnp.dot(g_vmem[b], part[m:], preferred_element_type=jnp.float32)
        out_ref[b] = basis.astype(out_ref.dtype)


def truncate_all(packed, scale, weights, left, right, rank):
    nb, n, _ = scale.shape
    small = pltpu.VMEM((nb, rank, rank), jnp.float32)
    big = pltpu.VMEM((nb, n, n), jnp.float32)
    vmem = pl.BlockSpec(memory_space=pltpu.VMEM)
    hbm = pl.BlockSpec(memory_space=pl.ANY)
    return pl.pallas_call(
        truncate_kernel,
        out_shape=(jax.ShapeDtypeStruct((nb, rank, rank), jnp.float32), jax.ShapeDtypeStruct(left.shape, left.dtype)),
        in_specs=[vmem, vmem, vmem, hbm, hbm],
        out_specs=(vmem, vmem),
        scratch_shapes=[small, small, small, small, big, big, big, pltpu.VMEM((nb, n, rank), jnp.float32),
                        pltpu.VMEM(left.shape, left.dtype), pltpu.VMEM(right.shape, right.dtype),
                        pltpu.SemaphoreType.DMA((2,))],
    )(packed, scale, weights, left, right)


def round_orders(needs):
    best = [list(bits) for bits in needs]

    def search(left, round_no, orders, budget):
        if all(not bits for bits in left):
            return orders
        if budget[0] <= 0:
            return None
        budget[0] -= 1
        active = sorted((i for i in range(len(left)) if left[i]), key=lambda i: -len(left[i]))

        def place(pos, used, picks):
            if pos == len(active):
                new_left = [list(bits) for bits in left]
                new_orders = [list(order) for order in orders]
                for i, bit in picks:
                    new_left[i].remove(bit)
                    new_orders[i].append(bit)
                return search(new_left, round_no + 1, new_orders, budget)
            i = active[pos]
            for bit in left[i]:
                link = bit if bit[0] == "gx" else ("gy",)
                if link not in used:
                    found = place(pos + 1, used | {link}, picks + [(i, bit)])
                    if found:
                        return found
            return None

        return place(0, frozenset(), [])

    found = search([list(bits) for bits in needs], 0, [[] for _ in needs], [2000])
    return found if found else best


def node_sums(items, needs):
    orders = round_orders([[bit for bit in bits if bit != ("gx", 0)] for bits in needs])
    core = lax.axis_index("gx") % 2
    half = items[0].shape[0] // 2
    out = []
    for item, order in zip(items, orders):
        low, high = item[:half], item[half:]
        mine = jnp.where(core == 0, low, high)
        mine = mine + swapped(jnp.where(core == 0, high, low), "gx", 0)
        for axis, bit in order:
            mine = mine + swapped(mine, axis, bit)
        other = swapped(mine, "gx", 0)
        out.append(jnp.where(core == 0, jnp.concatenate([mine, other], 0), jnp.concatenate([other, mine], 0)))
    return out


def pack(gram, rank):
    rows = lax.broadcasted_iota(jnp.int32, (rank, rank), 0)
    cols = lax.broadcasted_iota(jnp.int32, (rank, rank), 1)
    both = jnp.where(rows <= cols, gram[0][0], gram[1][1].T)
    diag = jnp.sum(jnp.where(rows == cols, gram[1][1], 0.0), axis=0, keepdims=True)
    pad = jnp.zeros((15, rank), jnp.float32)
    return jnp.concatenate([both, gram[0][1], diag, pad], axis=0)


def body(bases, gains, scales):
    rank = bases.shape[-1]
    local_rows = bases.shape[1] * bases.shape[2]
    bits_x = lax.axis_size("gx").bit_length() - 1
    bits_y = lax.axis_size("gy").bit_length() - 1
    left = bases.reshape(LEVELS, local_rows, rank)
    right = gains.reshape(LEVELS, local_rows, rank)
    packed = []
    needs = []
    sizes = []
    for k in range(LEVELS):
        groups = (bits_x - (k + 1) // 2, bits_y - k // 2)
        gram = [[jnp.dot(one.T, two, preferred_element_type=jnp.float32) for two in (left[k], right[k])] for one in (left[k], right[k])]
        packed.append(pack(lax.optimization_barrier(gram), rank))
        needs.append([("gx", bit) for bit in range(groups[0])] + [("gy", bit) for bit in range(groups[1])])
        sizes.append(local_rows * 2 ** (groups[0] + groups[1]))
    summed = jnp.stack(node_sums(packed, needs))
    n_rows = jnp.array(sizes, jnp.float32)[:, None, None]
    weights = scales[:, :, None]
    core, basis = truncate_all(summed, weights * tr(weights) / n_rows, tr(weights), left, right, rank)
    return (basis.reshape(bases.shape), core.reshape(LEVELS, 1, 1, rank, rank))


def solution(mesh):
    in_specs = (P(None, "gx", "gy", None), P(None, "gx", "gy", None), P())
    out_specs = (P(None, "gx", "gy", None), P(None, "gx", "gy", None, None))
    return jax.shard_map(body, mesh=mesh, in_specs=in_specs, out_specs=out_specs, check_vma=False)
```

```python
import jax
import jax.numpy as jnp
from jax import lax
from jax.experimental import pallas as pl
from jax.experimental.pallas import tpu as pltpu
from jax.sharding import PartitionSpec as P

LEVELS = 3


def swapped(block, axis, apart):
    count = lax.axis_size(axis)
    route = []
    for low in range(count):
        high = low | 1 << apart
        if high != low and high < count:
            route += [(low, high), (high, low)]
    return lax.ppermute(block, axis, route)


def tr(block):
    return jnp.swapaxes(block, -1, -2)


def dot(left, right):
    return jnp.dot(left, right, precision=lax.Precision.HIGHEST, preferred_element_type=jnp.float32)


def sym(block):
    return (block + block.T) / 2


def factor(ain, lt_ref, w_ref):
    nb, n, _ = ain.shape
    nt = n // 8
    lane = lax.broadcasted_iota(jnp.int32, (1, n), 1)
    sub8 = lax.broadcasted_iota(jnp.int32, (8, 1), 0)
    rows8 = lax.broadcasted_iota(jnp.int32, (8, n), 0)
    cols8 = lax.broadcasted_iota(jnp.int32, (8, n), 1)
    a = [[ain[b, 8 * u:8 * u + 8, :] for u in range(nt)] for b in range(nb)]
    w = [[jnp.where(cols8 == rows8 + 8 * u, 1.0, 0.0).astype(jnp.float32) for u in range(nt)] for b in range(nb)]
    lt = [[None] * nt for b in range(nb)]
    for j in range(n):
        u0, s = divmod(j, 8)
        for b in range(nb):
            rowj = a[b][u0][s:s + 1, :]
            r = lax.rsqrt(rowj[:, j:j + 1])
            lrow = jnp.where(lane >= j, rowj * r, 0.0)
            if s == 0:
                lt[b][u0] = jnp.broadcast_to(lrow, (8, n))
            else:
                lt[b][u0] = jnp.where(sub8 == s, lrow, lt[b][u0])
            xrow = w[b][u0][s:s + 1, :] * r
            for u in range(u0, nt):
                col = a[b][u][:, j:j + 1] * r
                if u == u0:
                    col = jnp.where(sub8 >= s, col, 0.0)
                    wcol = col - jnp.where(sub8 == s, 1.0, 0.0)
                else:
                    wcol = col
                a[b][u] = a[b][u] - col * lrow
                w[b][u] = w[b][u] - wcol * xrow
    for b in range(nb):
        for u in range(nt):
            lt_ref[b, 8 * u:8 * u + 8, :] = lt[b][u]
            w_ref[b, 8 * u:8 * u + 8, :] = w[b][u]


def truncate_kernel(p_ref, s_ref, w_ref, b_hbm, g_hbm, core_ref, out_ref, ain, lt, winv, l21, low, inv, kern, zed,
                    b_vmem, g_vmem, sems):
    nb, m, _ = ain.shape
    rows = lax.broadcasted_iota(jnp.int32, (m, m), 0)
    cols = lax.broadcasted_iota(jnp.int32, (m, m), 1)
    copies = [pltpu.make_async_copy(b_hbm, b_vmem, sems.at[0]), pltpu.make_async_copy(g_hbm, g_vmem, sems.at[1])]
    for copy in copies:
        copy.start()

    def stage(step, carry):
        @pl.when(step == 0)
        def _():
            for b in range(nb):
                both = p_ref[b, :m]
                ain[b] = jnp.where(rows <= cols, both, both.T) * s_ref[b, :m, :m]

        @pl.when(step == 1)
        def _():
            for b in range(nb):
                inv11 = winv[b]
                low[b, :m, :m] = lt[b].T
                low[b, :m, m:] = jnp.zeros((m, m), jnp.float32)
                inv[b, :m, :m] = inv11
                inv[b, :m, m:] = jnp.zeros((m, m), jnp.float32)
                both = p_ref[b, :m]
                lower = jnp.where(rows > cols, both, jnp.where(rows == cols, p_ref[b, 2 * m:2 * m + 1, :], both.T))
                low21 = dot(p_ref[b, m:2 * m].T * s_ref[b, m:, :m], inv11.T)
                l21[b] = low21
                low[b, m:, :m] = low21
                ain[b] = sym(lower * s_ref[b, m:, m:] - dot(low21, low21.T))

        @pl.when(step == 2)
        def _():
            for b in range(nb):
                inv22 = winv[b]
                low[b, m:, m:] = lt[b].T
                inv[b, m:, m:] = inv22
                inv[b, m:, :m] = -dot(inv22, dot(l21[b], inv[b, :m, :m]))
                full = low[b]
                kernel = dot(full.T, full)
                kern[b] = kernel
                first = kernel[:, :m]
                ain[b] = sym(dot(first.T, first))

        @pl.when(step == 3)
        def _():
            for b in range(nb):
                first_w = dot(kern[b, :, :m], winv[b].T)
                zz = dot(kern[b], first_w)
                zed[b] = zz
                ain[b] = sym(dot(zz.T, zz))

        factor(ain, lt, winv)
        return carry

    lax.fori_loop(0, 4, stage, 0)
    for copy in copies:
        copy.wait()
    for b in range(nb):
        second_w = dot(zed[b], winv[b].T)
        core_ref[b] = dot(dot(second_w.T, kern[b]), second_w)
        mixing = dot((inv[b] * w_ref[b]).T, second_w)
        basis = jnp.zeros(out_ref.shape[1:], jnp.float32)
        for _ in range(3):
            part = mixing.astype(jnp.bfloat16)
            mixing = mixing - part.astype(jnp.float32)
            basis = basis + jnp.dot(b_vmem[b], part[:m], preferred_element_type=jnp.float32)
            basis = basis + jnp.dot(g_vmem[b], part[m:], preferred_element_type=jnp.float32)
        out_ref[b] = basis.astype(out_ref.dtype)


def truncate_all(packed, scale, weights, left, right, rank):
    nb, n, _ = scale.shape
    small = pltpu.VMEM((nb, rank, rank), jnp.float32)
    big = pltpu.VMEM((nb, n, n), jnp.float32)
    vmem = pl.BlockSpec(memory_space=pltpu.VMEM)
    hbm = pl.BlockSpec(memory_space=pl.ANY)
    return pl.pallas_call(
        truncate_kernel,
        out_shape=(jax.ShapeDtypeStruct((nb, rank, rank), jnp.float32), jax.ShapeDtypeStruct(left.shape, left.dtype)),
        in_specs=[vmem, vmem, vmem, hbm, hbm],
        out_specs=(vmem, vmem),
        scratch_shapes=[small, small, small, small, big, big, big, pltpu.VMEM((nb, n, rank), jnp.float32),
                        pltpu.VMEM(left.shape, left.dtype), pltpu.VMEM(right.shape, right.dtype),
                        pltpu.SemaphoreType.DMA((2,))],
    )(packed, scale, weights, left, right)


def round_orders(needs):
    best = [list(bits) for bits in needs]

    def search(left, round_no, orders, budget):
        if all(not bits for bits in left):
            return orders
        if budget[0] <= 0:
            return None
        budget[0] -= 1
        active = sorted((i for i in range(len(left)) if left[i]), key=lambda i: -len(left[i]))

        def place(pos, used, picks):
            if pos == len(active):
                new_left = [list(bits) for bits in left]
                new_orders = [list(order) for order in orders]
                for i, bit in picks:
                    new_left[i].remove(bit)
                    new_orders[i].append(bit)
                return search(new_left, round_no + 1, new_orders, budget)
            i = active[pos]
            for bit in left[i]:
                link = bit
                if link not in used:
                    found = place(pos + 1, used | {link}, picks + [(i, bit)])
                    if found:
                        return found
            return None

        return place(0, frozenset(), [])

    found = search([list(bits) for bits in needs], 0, [[] for _ in needs], [2000])
    return found if found else best


def node_sums(items, needs):
    orders = round_orders([[bit for bit in bits if bit != ("gx", 0)] for bits in needs])
    core = lax.axis_index("gx") % 2
    half = items[0].shape[0] // 2
    out = []
    for item, order in zip(items, orders):
        low, high = item[:half], item[half:]
        mine = jnp.where(core == 0, low, high)
        mine = mine + swapped(jnp.where(core == 0, high, low), "gx", 0)
        for axis, bit in order:
            mine = mine + swapped(mine, axis, bit)
        other = swapped(mine, "gx", 0)
        out.append(jnp.where(core == 0, jnp.concatenate([mine, other], 0), jnp.concatenate([other, mine], 0)))
    return out


def pack(gram, rank):
    rows = lax.broadcasted_iota(jnp.int32, (rank, rank), 0)
    cols = lax.broadcasted_iota(jnp.int32, (rank, rank), 1)
    both = jnp.where(rows <= cols, gram[0][0], gram[1][1].T)
    diag = jnp.sum(jnp.where(rows == cols, gram[1][1], 0.0), axis=0, keepdims=True)
    pad = jnp.zeros((15, rank), jnp.float32)
    return jnp.concatenate([both, gram[0][1], diag, pad], axis=0)


def body(bases, gains, scales):
    rank = bases.shape[-1]
    local_rows = bases.shape[1] * bases.shape[2]
    bits_x = lax.axis_size("gx").bit_length() - 1
    bits_y = lax.axis_size("gy").bit_length() - 1
    left = bases.reshape(LEVELS, local_rows, rank)
    right = gains.reshape(LEVELS, local_rows, rank)
    packed = []
    needs = []
    sizes = []
    for k in range(LEVELS):
        groups = (bits_x - (k + 1) // 2, bits_y - k // 2)
        gram = [[jnp.dot(one.T, two, preferred_element_type=jnp.float32) for two in (left[k], right[k])] for one in (left[k], right[k])]
        packed.append(pack(lax.optimization_barrier(gram), rank))
        needs.append([("gx", bit) for bit in range(groups[0])] + [("gy", bit) for bit in range(groups[1])])
        sizes.append(local_rows * 2 ** (groups[0] + groups[1]))
    summed = jnp.stack(node_sums(packed, needs))
    n_rows = jnp.array(sizes, jnp.float32)[:, None, None]
    weights = scales[:, :, None]
    core, basis = truncate_all(summed, weights * tr(weights) / n_rows, tr(weights), left, right, rank)
    return (basis.reshape(bases.shape), core.reshape(LEVELS, 1, 1, rank, rank))


def solution(mesh):
    in_specs = (P(None, "gx", "gy", None), P(None, "gx", "gy", None), P())
    out_specs = (P(None, "gx", "gy", None), P(None, "gx", "gy", None, None))
    return jax.shard_map(body, mesh=mesh, in_specs=in_specs, out_specs=out_specs, check_vma=False)
```

```python
import jax
import jax.numpy as jnp
from jax import lax
from jax.experimental import pallas as pl
from jax.experimental.pallas import tpu as pltpu
from jax.sharding import PartitionSpec as P

LEVELS = 3


def swapped(block, axis, apart):
    count = lax.axis_size(axis)
    route = []
    for low in range(count):
        high = low | 1 << apart
        if high != low and high < count:
            route += [(low, high), (high, low)]
    return lax.ppermute(block, axis, route)


def tr(block):
    return jnp.swapaxes(block, -1, -2)


def dot(left, right):
    return jnp.dot(left, right, precision=lax.Precision.HIGHEST, preferred_element_type=jnp.float32)


def sym(block):
    return (block + block.T) / 2


def factor(ain, lt_ref, w_ref):
    nb, n, _ = ain.shape
    nt = n // 8
    lane = lax.broadcasted_iota(jnp.int32, (1, n), 1)
    sub8 = lax.broadcasted_iota(jnp.int32, (8, 1), 0)
    rows8 = lax.broadcasted_iota(jnp.int32, (8, n), 0)
    cols8 = lax.broadcasted_iota(jnp.int32, (8, n), 1)
    a = [[ain[b, 8 * u:8 * u + 8, :] for u in range(nt)] for b in range(nb)]
    w = [[jnp.where(cols8 == rows8 + 8 * u, 1.0, 0.0).astype(jnp.float32) for u in range(nt)] for b in range(nb)]
    lt = [[None] * nt for b in range(nb)]
    for j in range(n):
        u0, s = divmod(j, 8)
        for b in range(nb):
            rowj = a[b][u0][s:s + 1, :]
            r = lax.rsqrt(rowj[:, j:j + 1])
            lrow = jnp.where(lane >= j, rowj * r, 0.0)
            if s == 0:
                lt[b][u0] = jnp.broadcast_to(lrow, (8, n))
            else:
                lt[b][u0] = jnp.where(sub8 == s, lrow, lt[b][u0])
            xrow = w[b][u0][s:s + 1, :] * r
            for u in range(u0, nt):
                col = a[b][u][:, j:j + 1] * r
                if u == u0:
                    col = jnp.where(sub8 >= s, col, 0.0)
                    wcol = col - jnp.where(sub8 == s, 1.0, 0.0)
                else:
                    wcol = col
                a[b][u] = a[b][u] - col * lrow
                w[b][u] = w[b][u] - wcol * xrow
    for b in range(nb):
        for u in range(nt):
            lt_ref[b, 8 * u:8 * u + 8, :] = lt[b][u]
            w_ref[b, 8 * u:8 * u + 8, :] = w[b][u]


def truncate_kernel(p_ref, s_ref, w_ref, b_hbm, g_hbm, core_ref, out_ref, ain, lt, winv, l21, low, inv, kern, zed,
                    b_vmem, g_vmem, sems):
    nb, m, _ = ain.shape
    rows = lax.broadcasted_iota(jnp.int32, (m, m), 0)
    cols = lax.broadcasted_iota(jnp.int32, (m, m), 1)
    copies = [pltpu.make_async_copy(b_hbm, b_vmem, sems.at[0]), pltpu.make_async_copy(g_hbm, g_vmem, sems.at[1])]
    for copy in copies:
        copy.start()

    def stage(step, carry):
        @pl.when(step == 0)
        def _():
            for b in range(nb):
                both = p_ref[b, :m]
                ain[b] = jnp.where(rows <= cols, both, both.T) * s_ref[b, :m, :m]

        @pl.when(step == 1)
        def _():
            for b in range(nb):
                inv11 = winv[b]
                low[b, :m, :m] = lt[b].T
                low[b, :m, m:] = jnp.zeros((m, m), jnp.float32)
                inv[b, :m, :m] = inv11
                inv[b, :m, m:] = jnp.zeros((m, m), jnp.float32)
                both = p_ref[b, :m]
                lower = jnp.where(rows > cols, both, jnp.where(rows == cols, p_ref[b, 2 * m:2 * m + 1, :], both.T))
                low21 = dot(p_ref[b, m:2 * m].T * s_ref[b, m:, :m], inv11.T)
                l21[b] = low21
                low[b, m:, :m] = low21
                ain[b] = sym(lower * s_ref[b, m:, m:] - dot(low21, low21.T))

        @pl.when(step == 2)
        def _():
            for b in range(nb):
                inv22 = winv[b]
                low[b, m:, m:] = lt[b].T
                inv[b, m:, m:] = inv22
                inv[b, m:, :m] = -dot(inv22, dot(l21[b], inv[b, :m, :m]))
                full = low[b]
                kernel = dot(full.T, full)
                kern[b] = kernel
                first = kernel[:, :m]
                ain[b] = sym(dot(first.T, first))

        @pl.when(step == 3)
        def _():
            for b in range(nb):
                first_w = dot(kern[b, :, :m], winv[b].T)
                zz = dot(kern[b], first_w)
                zed[b] = zz
                ain[b] = sym(dot(zz.T, zz))

        factor(ain, lt, winv)
        return carry

    lax.fori_loop(0, 4, stage, 0)
    for copy in copies:
        copy.wait()
    for b in range(nb):
        second_w = dot(zed[b], winv[b].T)
        core_ref[b] = dot(dot(second_w.T, kern[b]), second_w)
        mixing = dot((inv[b] * w_ref[b]).T, second_w)
        basis = jnp.zeros(out_ref.shape[1:], jnp.float32)
        for _ in range(3):
            part = mixing.astype(jnp.bfloat16)
            mixing = mixing - part.astype(jnp.float32)
            basis = basis + jnp.dot(b_vmem[b], part[:m], preferred_element_type=jnp.float32)
            basis = basis + jnp.dot(g_vmem[b], part[m:], preferred_element_type=jnp.float32)
        out_ref[b] = basis.astype(out_ref.dtype)


def truncate_all(packed, scale, weights, left, right, rank):
    nb, n, _ = scale.shape
    small = pltpu.VMEM((nb, rank, rank), jnp.float32)
    big = pltpu.VMEM((nb, n, n), jnp.float32)
    vmem = pl.BlockSpec(memory_space=pltpu.VMEM)
    hbm = pl.BlockSpec(memory_space=pl.ANY)
    return pl.pallas_call(
        truncate_kernel,
        out_shape=(jax.ShapeDtypeStruct((nb, rank, rank), jnp.float32), jax.ShapeDtypeStruct(left.shape, left.dtype)),
        in_specs=[vmem, vmem, vmem, hbm, hbm],
        out_specs=(vmem, vmem),
        scratch_shapes=[small, small, small, small, big, big, big, pltpu.VMEM((nb, n, rank), jnp.float32),
                        pltpu.VMEM(left.shape, left.dtype), pltpu.VMEM(right.shape, right.dtype),
                        pltpu.SemaphoreType.DMA((2,))],
    )(packed, scale, weights, left, right)


def round_orders(needs):
    best = [list(bits) for bits in needs]

    def search(left, round_no, orders, budget):
        if all(not bits for bits in left):
            return orders
        if budget[0] <= 0:
            return None
        budget[0] -= 1
        active = sorted((i for i in range(len(left)) if left[i]), key=lambda i: -len(left[i]))

        def place(pos, used, picks):
            if pos == len(active):
                new_left = [list(bits) for bits in left]
                new_orders = [list(order) for order in orders]
                for i, bit in picks:
                    new_left[i].remove(bit)
                    new_orders[i].append(bit)
                return search(new_left, round_no + 1, new_orders, budget)
            i = active[pos]
            for bit in left[i]:
                link = bit if bit[0] == "gx" else ("gy",)
                if link not in used:
                    found = place(pos + 1, used | {link}, picks + [(i, bit)])
                    if found:
                        return found
            return None

        return place(0, frozenset(), [])

    found = search([list(bits) for bits in needs], 0, [[] for _ in needs], [2000])
    return found if found else best


def node_sums(items, needs):
    orders = round_orders([[bit for bit in bits if bit != ("gx", 0)] for bits in needs])
    core = lax.axis_index("gx") % 2
    half = items[0].shape[0] // 2
    out = []
    for item, order in zip(items, orders):
        low, high = item[:half], item[half:]
        mine = jnp.where(core == 0, low, high)
        mine = mine + swapped(jnp.where(core == 0, high, low), "gx", 0)
        for axis, bit in order:
            mine = mine + swapped(mine, axis, bit)
        other = swapped(mine, "gx", 0)
        out.append(jnp.where(core == 0, jnp.concatenate([mine, other], 0), jnp.concatenate([other, mine], 0)))
    return out


def pack(gram, rank):
    rows = lax.broadcasted_iota(jnp.int32, (rank, rank), 0)
    cols = lax.broadcasted_iota(jnp.int32, (rank, rank), 1)
    both = jnp.where(rows <= cols, gram[0][0], gram[1][1].T)
    diag = jnp.sum(jnp.where(rows == cols, gram[1][1], 0.0), axis=0, keepdims=True)
    pad = jnp.zeros((15, rank), jnp.float32)
    return jnp.concatenate([both, gram[0][1], diag, pad], axis=0)


def body(bases, gains, scales):
    rank = bases.shape[-1]
    local_rows = bases.shape[1] * bases.shape[2]
    bits_x = lax.axis_size("gx").bit_length() - 1
    bits_y = lax.axis_size("gy").bit_length() - 1
    left = bases.reshape(LEVELS, local_rows, rank)
    right = gains.reshape(LEVELS, local_rows, rank)
    packed = []
    needs = []
    sizes = []
    pair = (left[0], right[0])
    for k in range(LEVELS):
        groups = (bits_x - (k + 1) // 2, bits_y - k // 2)
        gram = [[jnp.dot(one.T, two, preferred_element_type=jnp.float32) for two in pair] for one in pair]
        item = pack(lax.optimization_barrier(gram), rank)
        if k + 1 < LEVELS:
            item, pair = lax.optimization_barrier((item, (left[k + 1], right[k + 1])))
        packed.append(item)
        needs.append([("gx", bit) for bit in range(groups[0])] + [("gy", bit) for bit in range(groups[1])])
        sizes.append(local_rows * 2 ** (groups[0] + groups[1]))
    summed = jnp.stack(node_sums(packed, needs))
    n_rows = jnp.array(sizes, jnp.float32)[:, None, None]
    weights = scales[:, :, None]
    core, basis = truncate_all(summed, weights * tr(weights) / n_rows, tr(weights), left, right, rank)
    return (basis.reshape(bases.shape), core.reshape(LEVELS, 1, 1, rank, rank))


def solution(mesh):
    in_specs = (P(None, "gx", "gy", None), P(None, "gx", "gy", None), P())
    out_specs = (P(None, "gx", "gy", None), P(None, "gx", "gy", None, None))
    return jax.shard_map(body, mesh=mesh, in_specs=in_specs, out_specs=out_specs, check_vma=False)
```

```python
import jax
import jax.numpy as jnp
from jax import lax
from jax.experimental import pallas as pl
from jax.experimental.pallas import tpu as pltpu
from jax.sharding import PartitionSpec as P

LEVELS = 3


def swapped(block, axis, apart):
    count = lax.axis_size(axis)
    route = []
    for low in range(count):
        high = low | 1 << apart
        if high != low and high < count:
            route += [(low, high), (high, low)]
    return lax.ppermute(block, axis, route)


def tr(block):
    return jnp.swapaxes(block, -1, -2)


def dot(left, right):
    return jnp.dot(left, right, precision=lax.Precision.HIGHEST, preferred_element_type=jnp.float32)


def sym(block):
    return (block + block.T) / 2


def factor(ain, lt_ref, w_ref):
    nb, n, _ = ain.shape
    nt = n // 8
    lane = lax.broadcasted_iota(jnp.int32, (1, n), 1)
    sub8 = lax.broadcasted_iota(jnp.int32, (8, 1), 0)
    rows8 = lax.broadcasted_iota(jnp.int32, (8, n), 0)
    cols8 = lax.broadcasted_iota(jnp.int32, (8, n), 1)
    a = [[ain[b, 8 * u:8 * u + 8, :] for u in range(nt)] for b in range(nb)]
    w = [[jnp.where(cols8 == rows8 + 8 * u, 1.0, 0.0).astype(jnp.float32) for u in range(nt)] for b in range(nb)]
    lt = [[None] * nt for b in range(nb)]
    for j in range(n):
        u0, s = divmod(j, 8)
        for b in range(nb):
            rowj = a[b][u0][s:s + 1, :]
            r = lax.rsqrt(rowj[:, j:j + 1])
            lrow = jnp.where(lane >= j, rowj * r, 0.0)
            if s == 0:
                lt[b][u0] = jnp.broadcast_to(lrow, (8, n))
            else:
                lt[b][u0] = jnp.where(sub8 == s, lrow, lt[b][u0])
            xrow = w[b][u0][s:s + 1, :] * r
            for u in range(u0, nt):
                col = a[b][u][:, j:j + 1] * r
                if u == u0:
                    col = jnp.where(sub8 >= s, col, 0.0)
                    wcol = col - jnp.where(sub8 == s, 1.0, 0.0)
                else:
                    wcol = col
                a[b][u] = a[b][u] - col * lrow
                w[b][u] = w[b][u] - wcol * xrow
    for b in range(nb):
        for u in range(nt):
            lt_ref[b, 8 * u:8 * u + 8, :] = lt[b][u]
            w_ref[b, 8 * u:8 * u + 8, :] = w[b][u]


def truncate_kernel(f_ref, m0, o0, m1, o1, m2, o2, s_ref, w_ref, b_hbm, g_hbm, core_ref, out_ref, ain, lt, winv, l21,
                    low, inv, kern, zed, b_vmem, g_vmem, sems):
    nb, m, _ = ain.shape
    rows = lax.broadcasted_iota(jnp.int32, (m, m), 0)
    cols = lax.broadcasted_iota(jnp.int32, (m, m), 1)
    halves = [(m0, o0), (m1, o1), (m2, o2)]

    def pieces(b):
        first = f_ref[...] > 0.5
        low_half = jnp.where(first, halves[b][0][...], halves[b][1][...])
        high_half = jnp.where(first, halves[b][1][...], halves[b][0][...])
        cross = jnp.concatenate([low_half[m:], high_half[:m - (low_half.shape[0] - m)]], 0)
        return low_half[:m], cross, high_half[m - (low_half.shape[0] - m):m - (low_half.shape[0] - m) + 1]

    copies = [pltpu.make_async_copy(b_hbm, b_vmem, sems.at[0]), pltpu.make_async_copy(g_hbm, g_vmem, sems.at[1])]
    for copy in copies:
        copy.start()

    def stage(step, carry):
        @pl.when(step == 0)
        def _():
            for b in range(nb):
                both = pieces(b)[0]
                ain[b] = jnp.where(rows <= cols, both, both.T) * s_ref[b, :m, :m]

        @pl.when(step == 1)
        def _():
            for b in range(nb):
                inv11 = winv[b]
                low[b, :m, :m] = lt[b].T
                low[b, :m, m:] = jnp.zeros((m, m), jnp.float32)
                inv[b, :m, :m] = inv11
                inv[b, :m, m:] = jnp.zeros((m, m), jnp.float32)
                both, cross, diag = pieces(b)
                lower = jnp.where(rows > cols, both, jnp.where(rows == cols, diag, both.T))
                low21 = dot(cross.T * s_ref[b, m:, :m], inv11.T)
                l21[b] = low21
                low[b, m:, :m] = low21
                ain[b] = sym(lower * s_ref[b, m:, m:] - dot(low21, low21.T))

        @pl.when(step == 2)
        def _():
            for b in range(nb):
                inv22 = winv[b]
                low[b, m:, m:] = lt[b].T
                inv[b, m:, m:] = inv22
                inv[b, m:, :m] = -dot(inv22, dot(l21[b], inv[b, :m, :m]))
                full = low[b]
                kernel = dot(full.T, full)
                kern[b] = kernel
                first = kernel[:, :m]
                ain[b] = sym(dot(first.T, first))

        @pl.when(step == 3)
        def _():
            for b in range(nb):
                first_w = dot(kern[b, :, :m], winv[b].T)
                zz = dot(kern[b], first_w)
                zed[b] = zz
                ain[b] = sym(dot(zz.T, zz))

        factor(ain, lt, winv)
        return carry

    lax.fori_loop(0, 4, stage, 0)
    for copy in copies:
        copy.wait()
    for b in range(nb):
        second_w = dot(zed[b], winv[b].T)
        core_ref[b] = dot(dot(second_w.T, kern[b]), second_w)
        mixing = dot((inv[b] * w_ref[b]).T, second_w)
        basis = jnp.zeros(out_ref.shape[1:], jnp.float32)
        for _ in range(3):
            part = mixing.astype(jnp.bfloat16)
            mixing = mixing - part.astype(jnp.float32)
            basis = basis + jnp.dot(b_vmem[b], part[:m], preferred_element_type=jnp.float32)
            basis = basis + jnp.dot(g_vmem[b], part[m:], preferred_element_type=jnp.float32)
        out_ref[b] = basis.astype(out_ref.dtype)


def truncate_all(flag, halves, scale, weights, left, right, rank):
    nb, n, _ = scale.shape
    small = pltpu.VMEM((nb, rank, rank), jnp.float32)
    big = pltpu.VMEM((nb, n, n), jnp.float32)
    vmem = pl.BlockSpec(memory_space=pltpu.VMEM)
    hbm = pl.BlockSpec(memory_space=pl.ANY)
    return pl.pallas_call(
        truncate_kernel,
        out_shape=(jax.ShapeDtypeStruct((nb, rank, rank), jnp.float32), jax.ShapeDtypeStruct(left.shape, left.dtype)),
        in_specs=[vmem] * 9 + [hbm, hbm],
        out_specs=(vmem, vmem),
        scratch_shapes=[small, small, small, small, big, big, big, pltpu.VMEM((nb, n, rank), jnp.float32),
                        pltpu.VMEM(left.shape, left.dtype), pltpu.VMEM(right.shape, right.dtype),
                        pltpu.SemaphoreType.DMA((2,))],
    )(flag, *[part for pair in halves for part in pair], scale, weights, left, right)


def round_orders(needs):
    best = [list(bits) for bits in needs]

    def search(left, round_no, orders, budget):
        if all(not bits for bits in left):
            return orders
        if budget[0] <= 0:
            return None
        budget[0] -= 1
        active = sorted((i for i in range(len(left)) if left[i]), key=lambda i: -len(left[i]))

        def place(pos, used, picks):
            if pos == len(active):
                new_left = [list(bits) for bits in left]
                new_orders = [list(order) for order in orders]
                for i, bit in picks:
                    new_left[i].remove(bit)
                    new_orders[i].append(bit)
                return search(new_left, round_no + 1, new_orders, budget)
            i = active[pos]
            for bit in left[i]:
                link = bit if bit[0] == "gx" else ("gy",)
                if link not in used:
                    found = place(pos + 1, used | {link}, picks + [(i, bit)])
                    if found:
                        return found
            return None

        return place(0, frozenset(), [])

    found = search([list(bits) for bits in needs], 0, [[] for _ in needs], [2000])
    return found if found else best


def node_sums(items, needs):
    orders = round_orders([[bit for bit in bits if bit != ("gx", 0)] for bits in needs])
    core = lax.axis_index("gx") % 2
    half = items[0].shape[0] // 2
    out = []
    for item, order in zip(items, orders):
        low, high = item[:half], item[half:]
        mine = jnp.where(core == 0, low, high)
        mine = mine + swapped(jnp.where(core == 0, high, low), "gx", 0)
        for axis, bit in order:
            mine = mine + swapped(mine, axis, bit)
        out.append((mine, swapped(mine, "gx", 0)))
    return out


def pack(gram, rank):
    rows = lax.broadcasted_iota(jnp.int32, (rank, rank), 0)
    cols = lax.broadcasted_iota(jnp.int32, (rank, rank), 1)
    both = jnp.where(rows <= cols, gram[0][0], gram[1][1].T)
    diag = jnp.sum(jnp.where(rows == cols, gram[1][1], 0.0), axis=0, keepdims=True)
    pad = jnp.zeros((15, rank), jnp.float32)
    return jnp.concatenate([both, gram[0][1], diag, pad], axis=0)


def body(bases, gains, scales):
    rank = bases.shape[-1]
    local_rows = bases.shape[1] * bases.shape[2]
    bits_x = lax.axis_size("gx").bit_length() - 1
    bits_y = lax.axis_size("gy").bit_length() - 1
    left = bases.reshape(LEVELS, local_rows, rank)
    right = gains.reshape(LEVELS, local_rows, rank)
    packed = []
    needs = []
    sizes = []
    for k in range(LEVELS):
        groups = (bits_x - (k + 1) // 2, bits_y - k // 2)
        gram = [[jnp.dot(one.T, two, preferred_element_type=jnp.float32) for two in (left[k], right[k])] for one in (left[k], right[k])]
        packed.append(pack(lax.optimization_barrier(gram), rank))
        needs.append([("gx", bit) for bit in range(groups[0])] + [("gy", bit) for bit in range(groups[1])])
        sizes.append(local_rows * 2 ** (groups[0] + groups[1]))
    halves = node_sums(packed, needs)
    flag = jnp.full((1, rank), lax.axis_index("gx") % 2 == 0, jnp.float32)
    n_rows = jnp.array(sizes, jnp.float32)[:, None, None]
    weights = scales[:, :, None]
    core, basis = truncate_all(flag, halves, weights * tr(weights) / n_rows, tr(weights), left, right, rank)
    return (basis.reshape(bases.shape), core.reshape(LEVELS, 1, 1, rank, rank))


def solution(mesh):
    in_specs = (P(None, "gx", "gy", None), P(None, "gx", "gy", None), P())
    out_specs = (P(None, "gx", "gy", None), P(None, "gx", "gy", None, None))
    return jax.shard_map(body, mesh=mesh, in_specs=in_specs, out_specs=out_specs, check_vma=False)
```

```python
import functools

import jax
import jax.numpy as jnp
from jax import lax
from jax.experimental import pallas as pl
from jax.experimental.pallas import tpu as pltpu
from jax.sharding import PartitionSpec as P

LEVELS = 3


def swapped(block, axis, apart):
    count = lax.axis_size(axis)
    route = []
    for low in range(count):
        high = low | 1 << apart
        if high != low and high < count:
            route += [(low, high), (high, low)]
    return lax.ppermute(block, axis, route)


def tr(block):
    return jnp.swapaxes(block, -1, -2)


def dot(left, right):
    return jnp.dot(left, right, precision=lax.Precision.HIGHEST, preferred_element_type=jnp.float32)


def sym(block):
    return (block + block.T) / 2


def factor(ain, lt_ref, w_ref):
    nb, n, _ = ain.shape
    nt = n // 8
    lane = lax.broadcasted_iota(jnp.int32, (1, n), 1)
    sub8 = lax.broadcasted_iota(jnp.int32, (8, 1), 0)
    rows8 = lax.broadcasted_iota(jnp.int32, (8, n), 0)
    cols8 = lax.broadcasted_iota(jnp.int32, (8, n), 1)
    a = [[ain[b, 8 * u:8 * u + 8, :] for u in range(nt)] for b in range(nb)]
    w = [[jnp.where(cols8 == rows8 + 8 * u, 1.0, 0.0).astype(jnp.float32) for u in range(nt)] for b in range(nb)]
    lt = [[None] * nt for b in range(nb)]
    for j in range(n):
        u0, s = divmod(j, 8)
        for b in range(nb):
            rowj = a[b][u0][s:s + 1, :]
            r = lax.rsqrt(rowj[:, j:j + 1])
            lrow = jnp.where(lane >= j, rowj * r, 0.0)
            if s == 0:
                lt[b][u0] = jnp.broadcast_to(lrow, (8, n))
            else:
                lt[b][u0] = jnp.where(sub8 == s, lrow, lt[b][u0])
            xrow = w[b][u0][s:s + 1, :] * r
            for u in range(u0, nt):
                col = a[b][u][:, j:j + 1] * r
                if u == u0:
                    col = jnp.where(sub8 >= s, col, 0.0)
                    wcol = col - jnp.where(sub8 == s, 1.0, 0.0)
                else:
                    wcol = col
                a[b][u] = a[b][u] - col * lrow
                w[b][u] = w[b][u] - wcol * xrow
    for b in range(nb):
        for u in range(nt):
            lt_ref[b, 8 * u:8 * u + 8, :] = lt[b][u]
            w_ref[b, 8 * u:8 * u + 8, :] = w[b][u]


def truncate_kernel(sizes, p_ref, c_ref, w_ref, b_hbm, g_hbm, core_ref, out_ref, ain, lt, winv, l21, low, inv, kern, zed,
                    b_vmem, g_vmem, sems):
    nb, m, _ = ain.shape
    rows = lax.broadcasted_iota(jnp.int32, (m, m), 0)
    cols = lax.broadcasted_iota(jnp.int32, (m, m), 1)
    copies = [pltpu.make_async_copy(b_hbm, b_vmem, sems.at[0]), pltpu.make_async_copy(g_hbm, g_vmem, sems.at[1])]
    for copy in copies:
        copy.start()

    def stage(step, carry):
        @pl.when(step == 0)
        def _():
            for b in range(nb):
                both = p_ref[b, :m]
                ain[b] = jnp.where(rows <= cols, both, both.T) * (c_ref[b, :m] * w_ref[b, :, :m] / sizes[b])

        @pl.when(step == 1)
        def _():
            for b in range(nb):
                inv11 = winv[b]
                low[b, :m, :m] = lt[b].T
                low[b, :m, m:] = jnp.zeros((m, m), jnp.float32)
                inv[b, :m, :m] = inv11
                inv[b, :m, m:] = jnp.zeros((m, m), jnp.float32)
                both = p_ref[b, :m]
                lower = jnp.where(rows > cols, both, jnp.where(rows == cols, p_ref[b, 2 * m:2 * m + 1, :], both.T))
                low21 = dot(p_ref[b, m:2 * m].T * (c_ref[b, m:] * w_ref[b, :, :m] / sizes[b]), inv11.T)
                l21[b] = low21
                low[b, m:, :m] = low21
                ain[b] = sym(lower * (c_ref[b, m:] * w_ref[b, :, m:] / sizes[b]) - dot(low21, low21.T))

        @pl.when(step == 2)
        def _():
            for b in range(nb):
                inv22 = winv[b]
                low[b, m:, m:] = lt[b].T
                inv[b, m:, m:] = inv22
                inv[b, m:, :m] = -dot(inv22, dot(l21[b], inv[b, :m, :m]))
                full = low[b]
                kernel = dot(full.T, full)
                kern[b] = kernel
                first = kernel[:, :m]
                ain[b] = sym(dot(first.T, first))

        @pl.when(step == 3)
        def _():
            for b in range(nb):
                first_w = dot(kern[b, :, :m], winv[b].T)
                zz = dot(kern[b], first_w)
                zed[b] = zz
                ain[b] = sym(dot(zz.T, zz))

        factor(ain, lt, winv)
        return carry

    lax.fori_loop(0, 4, stage, 0)
    for copy in copies:
        copy.wait()
    for b in range(nb):
        second_w = dot(zed[b], winv[b].T)
        core_ref[b] = dot(dot(second_w.T, kern[b]), second_w)
        mixing = dot((inv[b] * w_ref[b]).T, second_w)
        basis = jnp.zeros(out_ref.shape[1:], jnp.float32)
        for _ in range(3):
            part = mixing.astype(jnp.bfloat16)
            mixing = mixing - part.astype(jnp.float32)
            basis = basis + jnp.dot(b_vmem[b], part[:m], preferred_element_type=jnp.float32)
            basis = basis + jnp.dot(g_vmem[b], part[m:], preferred_element_type=jnp.float32)
        out_ref[b] = basis.astype(out_ref.dtype)


def truncate_all(packed, sizes, column, weights, left, right, rank):
    nb, n, _ = column.shape
    small = pltpu.VMEM((nb, rank, rank), jnp.float32)
    big = pltpu.VMEM((nb, n, n), jnp.float32)
    vmem = pl.BlockSpec(memory_space=pltpu.VMEM)
    hbm = pl.BlockSpec(memory_space=pl.ANY)
    return pl.pallas_call(
        functools.partial(truncate_kernel, sizes),
        out_shape=(jax.ShapeDtypeStruct((nb, rank, rank), jnp.float32), jax.ShapeDtypeStruct(left.shape, left.dtype)),
        in_specs=[vmem, vmem, vmem, hbm, hbm],
        out_specs=(vmem, vmem),
        scratch_shapes=[small, small, small, small, big, big, big, pltpu.VMEM((nb, n, rank), jnp.float32),
                        pltpu.VMEM(left.shape, left.dtype), pltpu.VMEM(right.shape, right.dtype),
                        pltpu.SemaphoreType.DMA((2,))],
    )(packed, column, weights, left, right)


def round_orders(needs):
    best = [list(bits) for bits in needs]

    def search(left, round_no, orders, budget):
        if all(not bits for bits in left):
            return orders
        if budget[0] <= 0:
            return None
        budget[0] -= 1
        active = sorted((i for i in range(len(left)) if left[i]), key=lambda i: -len(left[i]))

        def place(pos, used, picks):
            if pos == len(active):
                new_left = [list(bits) for bits in left]
                new_orders = [list(order) for order in orders]
                for i, bit in picks:
                    new_left[i].remove(bit)
                    new_orders[i].append(bit)
                return search(new_left, round_no + 1, new_orders, budget)
            i = active[pos]
            for bit in left[i]:
                link = bit if bit[0] == "gx" else ("gy",)
                if link not in used:
                    found = place(pos + 1, used | {link}, picks + [(i, bit)])
                    if found:
                        return found
            return None

        return place(0, frozenset(), [])

    found = search([list(bits) for bits in needs], 0, [[] for _ in needs], [2000])
    return found if found else best


def node_sums(items, needs):
    orders = round_orders([[bit for bit in bits if bit != ("gx", 0)] for bits in needs])
    core = lax.axis_index("gx") % 2
    half = items[0].shape[0] // 2
    out = []
    for item, order in zip(items, orders):
        low, high = item[:half], item[half:]
        mine = jnp.where(core == 0, low, high)
        mine = mine + swapped(jnp.where(core == 0, high, low), "gx", 0)
        for axis, bit in order:
            mine = mine + swapped(mine, axis, bit)
        other = swapped(mine, "gx", 0)
        out.append(jnp.where(core == 0, jnp.concatenate([mine, other], 0), jnp.concatenate([other, mine], 0)))
    return out


def pack(gram, rank):
    rows = lax.broadcasted_iota(jnp.int32, (rank, rank), 0)
    cols = lax.broadcasted_iota(jnp.int32, (rank, rank), 1)
    both = jnp.where(rows <= cols, gram[0][0], gram[1][1].T)
    diag = jnp.sum(jnp.where(rows == cols, gram[1][1], 0.0), axis=0, keepdims=True)
    pad = jnp.zeros((15, rank), jnp.float32)
    return jnp.concatenate([both, gram[0][1], diag, pad], axis=0)


def body(bases, gains, scales):
    rank = bases.shape[-1]
    local_rows = bases.shape[1] * bases.shape[2]
    bits_x = lax.axis_size("gx").bit_length() - 1
    bits_y = lax.axis_size("gy").bit_length() - 1
    left = bases.reshape(LEVELS, local_rows, rank)
    right = gains.reshape(LEVELS, local_rows, rank)
    packed = []
    needs = []
    sizes = []
    for k in range(LEVELS):
        groups = (bits_x - (k + 1) // 2, bits_y - k // 2)
        gram = [[jnp.dot(one.T, two, preferred_element_type=jnp.float32) for two in (left[k], right[k])] for one in (left[k], right[k])]
        packed.append(pack(lax.optimization_barrier(gram), rank))
        needs.append([("gx", bit) for bit in range(groups[0])] + [("gy", bit) for bit in range(groups[1])])
        sizes.append(local_rows * 2 ** (groups[0] + groups[1]))
    summed = jnp.stack(node_sums(packed, needs))
    weights = scales[:, :, None]
    core, basis = truncate_all(summed, tuple(float(size) for size in sizes), weights, tr(weights), left, right, rank)
    return (basis.reshape(bases.shape), core.reshape(LEVELS, 1, 1, rank, rank))


def solution(mesh):
    in_specs = (P(None, "gx", "gy", None), P(None, "gx", "gy", None), P())
    out_specs = (P(None, "gx", "gy", None), P(None, "gx", "gy", None, None))
    return jax.shard_map(body, mesh=mesh, in_specs=in_specs, out_specs=out_specs, check_vma=False)
```

```python
import jax
import jax.numpy as jnp
from jax import lax
from jax.experimental import pallas as pl
from jax.experimental.pallas import tpu as pltpu
from jax.sharding import PartitionSpec as P

LEVELS = 3


def swapped(block, axis, apart):
    count = lax.axis_size(axis)
    route = []
    for low in range(count):
        high = low | 1 << apart
        if high != low and high < count:
            route += [(low, high), (high, low)]
    return lax.ppermute(block, axis, route)


def tr(block):
    return jnp.swapaxes(block, -1, -2)


def dot(left, right):
    return jnp.dot(left, right, precision=lax.Precision.HIGHEST, preferred_element_type=jnp.float32)


def factor(ain, lt_ref, w_ref):
    nb, n, _ = ain.shape
    nt = n // 8
    lane = lax.broadcasted_iota(jnp.int32, (1, n), 1)
    sub8 = lax.broadcasted_iota(jnp.int32, (8, 1), 0)
    rows8 = lax.broadcasted_iota(jnp.int32, (8, n), 0)
    cols8 = lax.broadcasted_iota(jnp.int32, (8, n), 1)
    a = [[ain[b, 8 * u:8 * u + 8, :] for u in range(nt)] for b in range(nb)]
    w = [[jnp.where(cols8 == rows8 + 8 * u, 1.0, 0.0).astype(jnp.float32) for u in range(nt)] for b in range(nb)]
    lt = [[None] * nt for b in range(nb)]
    for j in range(n):
        u0, s = divmod(j, 8)
        for b in range(nb):
            rowj = a[b][u0][s:s + 1, :]
            r = lax.rsqrt(rowj[:, j:j + 1])
            lrow = jnp.where(lane >= j, rowj * r, 0.0)
            if s == 0:
                lt[b][u0] = jnp.broadcast_to(lrow, (8, n))
            else:
                lt[b][u0] = jnp.where(sub8 == s, lrow, lt[b][u0])
            xrow = w[b][u0][s:s + 1, :] * r
            for u in range(u0, nt):
                col = a[b][u][:, j:j + 1] * r
                if u == u0:
                    col = jnp.where(sub8 >= s, col, 0.0)
                    wcol = col - jnp.where(sub8 == s, 1.0, 0.0)
                else:
                    wcol = col
                a[b][u] = a[b][u] - col * lrow
                w[b][u] = w[b][u] - wcol * xrow
    for b in range(nb):
        for u in range(nt):
            lt_ref[b, 8 * u:8 * u + 8, :] = lt[b][u]
            w_ref[b, 8 * u:8 * u + 8, :] = w[b][u]


def truncate_kernel(p_ref, s_ref, w_ref, b_hbm, g_hbm, core_ref, out_ref, ain, lt, winv, l21, low, inv, kern, zed,
                    b_vmem, g_vmem, sems):
    nb, m, _ = ain.shape
    rows = lax.broadcasted_iota(jnp.int32, (m, m), 0)
    cols = lax.broadcasted_iota(jnp.int32, (m, m), 1)
    copies = [pltpu.make_async_copy(b_hbm, b_vmem, sems.at[0]), pltpu.make_async_copy(g_hbm, g_vmem, sems.at[1])]
    for copy in copies:
        copy.start()

    def stage(step, carry):
        @pl.when(step == 0)
        def _():
            for b in range(nb):
                both = p_ref[b, :m]
                ain[b] = jnp.where(rows <= cols, both, both.T) * s_ref[b, :m, :m]

        @pl.when(step == 1)
        def _():
            for b in range(nb):
                inv11 = winv[b]
                low[b, :m, :m] = lt[b].T
                low[b, :m, m:] = jnp.zeros((m, m), jnp.float32)
                inv[b, :m, :m] = inv11
                inv[b, :m, m:] = jnp.zeros((m, m), jnp.float32)
                both = p_ref[b, :m]
                lower = jnp.where(rows > cols, both, jnp.where(rows == cols, p_ref[b, 2 * m:2 * m + 1, :], both.T))
                low21 = dot(p_ref[b, m:2 * m].T * s_ref[b, m:, :m], inv11.T)
                l21[b] = low21
                low[b, m:, :m] = low21
                ain[b] = lower * s_ref[b, m:, m:] - dot(low21, low21.T)

        @pl.when(step == 2)
        def _():
            for b in range(nb):
                inv22 = winv[b]
                low[b, m:, m:] = lt[b].T
                inv[b, m:, m:] = inv22
                inv[b, m:, :m] = -dot(inv22, dot(l21[b], inv[b, :m, :m]))
                full = low[b]
                kernel = dot(full.T, full)
                kern[b] = kernel
                first = kernel[:, :m]
                ain[b] = dot(first.T, first)

        @pl.when(step == 3)
        def _():
            for b in range(nb):
                first_w = dot(kern[b, :, :m], winv[b].T)
                zz = dot(kern[b], first_w)
                zed[b] = zz
                ain[b] = dot(zz.T, zz)

        factor(ain, lt, winv)
        return carry

    lax.fori_loop(0, 4, stage, 0)
    for copy in copies:
        copy.wait()
    for b in range(nb):
        second_w = dot(zed[b], winv[b].T)
        core_ref[b] = dot(dot(second_w.T, kern[b]), second_w)
        mixing = dot((inv[b] * w_ref[b]).T, second_w)
        basis = jnp.zeros(out_ref.shape[1:], jnp.float32)
        for _ in range(3):
            part = mixing.astype(jnp.bfloat16)
            mixing = mixing - part.astype(jnp.float32)
            basis = basis + jnp.dot(b_vmem[b], part[:m], preferred_element_type=jnp.float32)
            basis = basis + jnp.dot(g_vmem[b], part[m:], preferred_element_type=jnp.float32)
        out_ref[b] = basis.astype(out_ref.dtype)


def truncate_all(packed, scale, weights, left, right, rank):
    nb, n, _ = scale.shape
    small = pltpu.VMEM((nb, rank, rank), jnp.float32)
    big = pltpu.VMEM((nb, n, n), jnp.float32)
    vmem = pl.BlockSpec(memory_space=pltpu.VMEM)
    hbm = pl.BlockSpec(memory_space=pl.ANY)
    return pl.pallas_call(
        truncate_kernel,
        out_shape=(jax.ShapeDtypeStruct((nb, rank, rank), jnp.float32), jax.ShapeDtypeStruct(left.shape, left.dtype)),
        in_specs=[vmem, vmem, vmem, hbm, hbm],
        out_specs=(vmem, vmem),
        scratch_shapes=[small, small, small, small, big, big, big, pltpu.VMEM((nb, n, rank), jnp.float32),
                        pltpu.VMEM(left.shape, left.dtype), pltpu.VMEM(right.shape, right.dtype),
                        pltpu.SemaphoreType.DMA((2,))],
    )(packed, scale, weights, left, right)


def round_orders(needs):
    best = [list(bits) for bits in needs]

    def search(left, round_no, orders, budget):
        if all(not bits for bits in left):
            return orders
        if budget[0] <= 0:
            return None
        budget[0] -= 1
        active = sorted((i for i in range(len(left)) if left[i]), key=lambda i: -len(left[i]))

        def place(pos, used, picks):
            if pos == len(active):
                new_left = [list(bits) for bits in left]
                new_orders = [list(order) for order in orders]
                for i, bit in picks:
                    new_left[i].remove(bit)
                    new_orders[i].append(bit)
                return search(new_left, round_no + 1, new_orders, budget)
            i = active[pos]
            for bit in left[i]:
                link = bit if bit[0] == "gx" else ("gy",)
                if link not in used:
                    found = place(pos + 1, used | {link}, picks + [(i, bit)])
                    if found:
                        return found
            return None

        return place(0, frozenset(), [])

    found = search([list(bits) for bits in needs], 0, [[] for _ in needs], [2000])
    return found if found else best


def node_sums(items, needs):
    orders = round_orders([[bit for bit in bits if bit != ("gx", 0)] for bits in needs])
    core = lax.axis_index("gx") % 2
    half = items[0].shape[0] // 2
    out = []
    for item, order in zip(items, orders):
        low, high = item[:half], item[half:]
        mine = jnp.where(core == 0, low, high)
        mine = mine + swapped(jnp.where(core == 0, high, low), "gx", 0)
        for axis, bit in order:
            mine = mine + swapped(mine, axis, bit)
        other = swapped(mine, "gx", 0)
        out.append(jnp.where(core == 0, jnp.concatenate([mine, other], 0), jnp.concatenate([other, mine], 0)))
    return out


def pack(gram, rank):
    rows = lax.broadcasted_iota(jnp.int32, (rank, rank), 0)
    cols = lax.broadcasted_iota(jnp.int32, (rank, rank), 1)
    both = jnp.where(rows <= cols, gram[0][0], gram[1][1].T)
    diag = jnp.sum(jnp.where(rows == cols, gram[1][1], 0.0), axis=0, keepdims=True)
    pad = jnp.zeros((15, rank), jnp.float32)
    return jnp.concatenate([both, gram[0][1], diag, pad], axis=0)


def body(bases, gains, scales):
    rank = bases.shape[-1]
    local_rows = bases.shape[1] * bases.shape[2]
    bits_x = lax.axis_size("gx").bit_length() - 1
    bits_y = lax.axis_size("gy").bit_length() - 1
    left = bases.reshape(LEVELS, local_rows, rank)
    right = gains.reshape(LEVELS, local_rows, rank)
    packed = []
    needs = []
    sizes = []
    for k in range(LEVELS):
        groups = (bits_x - (k + 1) // 2, bits_y - k // 2)
        gram = [[jnp.dot(one.T, two, preferred_element_type=jnp.float32) for two in (left[k], right[k])] for one in (left[k], right[k])]
        packed.append(pack(lax.optimization_barrier(gram), rank))
        needs.append([("gx", bit) for bit in range(groups[0])] + [("gy", bit) for bit in range(groups[1])])
        sizes.append(local_rows * 2 ** (groups[0] + groups[1]))
    summed = jnp.stack(node_sums(packed, needs))
    n_rows = jnp.array(sizes, jnp.float32)[:, None, None]
    weights = scales[:, :, None]
    core, basis = truncate_all(summed, weights * tr(weights) / n_rows, tr(weights), left, right, rank)
    return (basis.reshape(bases.shape), core.reshape(LEVELS, 1, 1, rank, rank))


def solution(mesh):
    in_specs = (P(None, "gx", "gy", None), P(None, "gx", "gy", None), P())
    out_specs = (P(None, "gx", "gy", None), P(None, "gx", "gy", None, None))
    return jax.shard_map(body, mesh=mesh, in_specs=in_specs, out_specs=out_specs, check_vma=False)
```
